32 devices in a mesh: dom: 4 (over y, x), grp: 8 (over z, core).
Axes of the slice: x: 2, y: 2, z: 4, core: 2. Of those that a mesh axis runs over, the one named last changes fastest.
Arguments:
- features: bfloat16 [40960, 128], P(('dom', 'grp')), may hold values from -6 to 6
- send_dom: int32 [32, 4, 32], P(('dom', 'grp')), may hold values from 0 to 1279
- send_grp: int32 [32, 8, 32], P(('dom', 'grp')), may hold values from 0 to 1279
- tile_vals: bfloat16 [1536, 128, 128], P(('dom', 'grp')), may hold values from 0.049804688 to 1
- tile_tgt: int32 [1536], P(('dom', 'grp')), may hold values from 0 to 9, as said below
- tile_src: int32 [1536], P(('dom', 'grp')), may hold values from 0 to 12, as said below
- tile_count: int32 [32], P(('dom', 'grp')), may hold values from 13 to 48, as said below
- w_self: bfloat16 [128, 256], replicated, may hold values from -0.5 to 0.5
- w_neigh: bfloat16 [128, 256], replicated, may hold values from -0.5 to 0.5
- cotangent: bfloat16 [40960, 256], P(('dom', 'grp'))
Outputs:
- output: bfloat16 [40960, 256], P(('dom', 'grp'))
- grad_features: bfloat16 [40960, 128], P(('dom', 'grp'))
- grad_self: float32 [128, 256], replicated
- grad_neigh: float32 [128, 256], replicated
The draws below stay inside these ranges and needn't reach their ends.
Inputs may be any that keep to these rules, and one draw needn't show every extreme that they name: `tile_tgt`: in every partition, tile slot t for t < 10 has target block t; other slots name any target block. `tile_src`: in every partition, tile slot t for t < 13 has source block t; other slots name any source block. `tile_count`: some partition has all 48 slots live in every draw.
All inputs are finite; a program needn't handle non-finite values.
Results may differ from the reference program's by a relative error of at most 0.0049.
Values may be sent and summed in bfloat16 or wider, within the bound.
No kernel may reach another device: no remote copies, remote signals or barrier semaphores. Data moves between devices by JAX's collectives and lax.ppermute only.
A program may use at most 64 MiB of HBM per device.

```python
import jax
import jax.numpy as jnp
from jax import lax

F = 128
H = 256
TILE = 128
NODES_DEV = 1280
BND = 32
TILES_MAX = 48
NB = 10
RB = 3
SB = 13
NODES = 40960
TILES_ALL = 1536
N_DOM = 4
N_GRP = 8
DEVICES = 32


def tile_layout(key):
    base = jax.random.fold_in(key, 7)
    first, second = jax.random.split(base)
    slots = jnp.broadcast_to(jnp.arange(TILES_MAX, dtype=jnp.int32)[None, :], (DEVICES, TILES_MAX))
    random_tgt = jax.random.randint(first, (DEVICES, TILES_MAX), 0, NB, dtype=jnp.int32)
    random_src = jax.random.randint(second, (DEVICES, TILES_MAX), 0, SB, dtype=jnp.int32)
    targets = jnp.where(slots < NB, slots, random_tgt)
    sources = jnp.where(slots < NB + RB, slots, random_src)
    return (targets.reshape(-1), sources.reshape(-1))


def draw_tile_tgt(key, part):
    return tile_layout(key)[0]


def draw_tile_src(key, part):
    return tile_layout(key)[1]


def draw_tile_count(key, part):
    counts = jax.random.randint(jax.random.fold_in(key, 11), (DEVICES,), NB + RB, TILES_MAX + 1, dtype=jnp.int32)
    busiest = jax.random.randint(jax.random.fold_in(key, 12), (), 0, DEVICES, dtype=jnp.int32)
    return counts.at[busiest].set(TILES_MAX)


def draw_cotangent(key, part):
    first = jax.random.fold_in(jax.random.fold_in(key, 21), 0)
    device = (jnp.arange(NODES, dtype=jnp.int32) // NODES_DEV).astype(jnp.float32)
    rise = 1.0 + 2.0 * device / max(DEVICES - 1, 1)
    base = jnp.clip(jax.random.normal(first, (NODES, H), jnp.float32), -6.0, 6.0)
    return (base * rise[:, None]).astype(jnp.bfloat16)


def place_ends(drawn, key, smallest, largest):
    spot = [jax.random.randint(jax.random.fold_in(key, axis), (), 0, length) for axis, length in enumerate(drawn.shape)]
    main_axis = drawn.shape.index(max(drawn.shape))
    beside = spot[:main_axis] + [(spot[main_axis] + 1) % drawn.shape[main_axis]] + spot[main_axis + 1:]
    return drawn.at[tuple(spot)].set(smallest).at[tuple(beside)].set(largest)


def block_levels(rng, extent, cuts, smallest, top_value):
    def one(axis_at, shards_of):
        heights = jax.random.uniform(jax.random.fold_in(jax.random.fold_in(rng, 6), axis_at), (shards_of,), jnp.float32, smallest / len(cuts), top_value / len(cuts))
        return jnp.repeat(jnp.exp(heights), extent[axis_at] // shards_of).reshape((-1,) + (1,) * (len(extent) - axis_at - 1))

    level = one(*cuts[0])
    for cut in cuts[1:]:
        level = level * one(*cut)
    return level


def gaussian(key, dims, deviation, limit, shards=(), kind=jnp.bfloat16):
    factor_of = block_levels(key, dims, shards, -0.22, 0.18) if shards else 1.0
    array = jax.random.normal(key, dims, jnp.float32) * deviation * factor_of
    return jnp.minimum(jnp.maximum(array, -limit), limit).astype(kind)


def setup_inputs(seed: int = 0) -> dict:
    arg_keys = jax.random.split(jax.random.key(seed), 11)
    return {
        "features": gaussian(arg_keys[0], (NODES, F), 1.0, 6.0, ((0, 32),)),
        "send_dom": place_ends(jax.random.randint(arg_keys[1], (DEVICES, N_DOM, BND), 0, NODES_DEV), jax.random.fold_in(arg_keys[1], 1), 0, NODES_DEV - 1).astype(jnp.int32),
        "send_grp": place_ends(jax.random.randint(arg_keys[2], (DEVICES, N_GRP, BND), 0, NODES_DEV), jax.random.fold_in(arg_keys[2], 1), 0, NODES_DEV - 1).astype(jnp.int32),
        "tile_vals": jnp.clip(0.049804688 + 0.9501953 * jax.random.uniform(arg_keys[3], (TILES_ALL, TILE, TILE), jnp.float32) ** block_levels(arg_keys[3], (TILES_ALL, TILE, TILE), ((0, 32),), -0.2, 0.2), 0.049804688, 1.0).astype(jnp.bfloat16),
        "tile_tgt": draw_tile_tgt(jax.random.fold_in(arg_keys[10], 71), 0),
        "tile_src": draw_tile_src(jax.random.fold_in(arg_keys[10], 71), 0),
        "tile_count": draw_tile_count(jax.random.fold_in(arg_keys[10], 71), 0),
        "w_self": gaussian(arg_keys[7], (F, H), F ** -0.5, 0.5),
        "w_neigh": gaussian(arg_keys[8], (F, H), F ** -0.5, 0.5),
        "cotangent": draw_cotangent(jax.random.fold_in(arg_keys[10], 71), 0),
    }


def reference(features, send_dom, send_grp, tile_vals, tile_tgt, tile_src, tile_count, w_self, w_neigh, cotangent):
    features_all = features.reshape(DEVICES, NODES_DEV, F)
    cot_all = cotangent.reshape(DEVICES, NODES_DEV, H)
    tiles_all = tile_vals.reshape(DEVICES, TILES_MAX, TILE, TILE)
    targets_all = tile_tgt.reshape(DEVICES, TILES_MAX)
    sources_all = tile_src.reshape(DEVICES, TILES_MAX)

    def device_pass(carry, device):
        domain = device // N_GRP
        group = device % N_GRP
        dom_peers = jnp.arange(N_DOM, dtype=jnp.int32) * N_GRP + group
        grp_peers = domain * N_GRP + jnp.arange(N_GRP, dtype=jnp.int32)
        dom_rows = features_all[dom_peers[:, None], send_dom[dom_peers, domain]]
        grp_rows = features_all[grp_peers[:, None], send_grp[grp_peers, group]]
        own = features_all[device]
        source = jnp.concatenate([own, dom_rows.reshape(-1, F), grp_rows.reshape(-1, F)], axis=0).reshape(SB, TILE, F)
        tiles = tiles_all[device].astype(jnp.float32)
        targets = targets_all[device]
        sources = sources_all[device]
        usable = (jnp.arange(TILES_MAX, dtype=jnp.int32) < tile_count[device]).astype(jnp.float32)
        products = jnp.einsum('tij,tjf->tif', tiles, source[sources].astype(jnp.float32)) * usable[:, None, None]
        summed = jax.ops.segment_sum(products, targets, num_segments=NB)
        degree = jax.ops.segment_sum(jnp.sum(tiles, axis=2) * usable[:, None], targets, num_segments=NB)
        agg = (summed / degree[:, :, None]).reshape(NODES_DEV, F).astype(jnp.bfloat16)
        preact = jnp.dot(own, w_self, preferred_element_type=jnp.float32) + jnp.dot(agg, w_neigh, preferred_element_type=jnp.float32)
        sigm = jax.nn.sigmoid(preact)
        output = (preact * sigm).astype(jnp.bfloat16)
        grad_pre = (cot_all[device].astype(jnp.float32) * sigm * (1.0 + preact * (1.0 - sigm))).astype(jnp.bfloat16)
        part_self = jnp.dot(own.T, grad_pre, preferred_element_type=jnp.float32)
        part_neigh = jnp.dot(agg.T, grad_pre, preferred_element_type=jnp.float32)
        grad_own = jnp.dot(grad_pre, w_self.T, preferred_element_type=jnp.float32)
        grad_agg = (jnp.dot(grad_pre, w_neigh.T, preferred_element_type=jnp.float32) / degree.reshape(-1)[:, None]).astype(jnp.bfloat16)
        picked = grad_agg.reshape(NB, TILE, F)[targets].astype(jnp.float32)
        backward = jnp.einsum('tij,tif->tjf', tiles, picked) * usable[:, None, None]
        grad_source = jax.ops.segment_sum(backward, sources, num_segments=SB).reshape(SB * TILE, F)
        local_grad = grad_own + grad_source[:NODES_DEV]
        remote = grad_source[NODES_DEV:].astype(jnp.bfloat16)
        return (carry[0] + part_self, carry[1] + part_neigh), (output, local_grad, remote)

    start = (jnp.zeros((F, H), jnp.float32), jnp.zeros((F, H), jnp.float32))
    sums, stacked = lax.scan(device_pass, start, jnp.arange(DEVICES, dtype=jnp.int32))
    outputs, local_grads, remotes = stacked
    remote_dom = remotes[:, :N_DOM * BND].reshape(DEVICES, N_DOM, BND, F)
    remote_grp = remotes[:, N_DOM * BND:].reshape(DEVICES, N_GRP, BND, F)

    def collect(owner):
        domain = owner // N_GRP
        group = owner % N_GRP
        from_dom = remote_dom[jnp.arange(N_DOM, dtype=jnp.int32) * N_GRP + group, domain].astype(jnp.float32)
        from_grp = remote_grp[domain * N_GRP + jnp.arange(N_GRP, dtype=jnp.int32), group].astype(jnp.float32)
        total = local_grads[owner]
        total = total.at[send_dom[owner].reshape(-1)].add(from_dom.reshape(-1, F))
        total = total.at[send_grp[owner].reshape(-1)].add(from_grp.reshape(-1, F))
        return total.astype(jnp.bfloat16)

    grad_features = lax.map(collect, jnp.arange(DEVICES, dtype=jnp.int32)).reshape(NODES, F)
    return outputs.reshape(NODES, H), grad_features, sums[0], sums[1]
```

```python
import jax
import jax.numpy as jnp
from jax import lax
from jax.sharding import PartitionSpec as P


def weight_sum(part_self, part_neigh):
    axes = ("dom", "grp")
    peers = lax.psum(1, axes)
    rows = part_self.shape[0]
    stacked = jnp.concatenate([part_self, part_neigh], axis=0)
    flat = stacked.reshape(-1)
    pad = (-flat.shape[0]) % peers
    chunks = jnp.pad(flat, (0, pad)).reshape(peers, -1)
    mine = jnp.sum(lax.all_to_all(chunks, axes, 0, 0, tiled=True), axis=0, keepdims=True)
    spread = jnp.broadcast_to(mine, chunks.shape)
    total = lax.all_to_all(spread, axes, 0, 0, tiled=True).reshape(-1)
    total = total[: flat.shape[0]].reshape(stacked.shape)
    return total[:rows], total[rows:]


def per_device(
    features,
    send_dom,
    send_grp,
    tile_vals,
    tile_tgt,
    tile_src,
    tile_count,
    w_self,
    w_neigh,
    cotangent,
):
    tile_size = tile_vals.shape[1]
    width = features.shape[1]
    node_count = features.shape[0]
    block_count = node_count // tile_size
    dom_index = send_dom[0]
    grp_index = send_grp[0]
    dom_peers = dom_index.shape[0]
    recv_dom = lax.all_to_all(features[dom_index], "dom", split_axis=0, concat_axis=0, tiled=True)
    recv_grp = lax.all_to_all(features[grp_index], "grp", split_axis=0, concat_axis=0, tiled=True)
    source = jnp.concatenate(
        [features, recv_dom.reshape(-1, width), recv_grp.reshape(-1, width)], axis=0
    )
    source = source.reshape(-1, tile_size, width)
    source_count = source.shape[0]
    slot_count = tile_vals.shape[0]
    usable = jnp.arange(slot_count, dtype=jnp.int32) < tile_count[0]
    to_target = (
        (tile_tgt[None, :] == jnp.arange(block_count, dtype=jnp.int32)[:, None]) & usable[None, :]
    ).astype(jnp.float32)
    to_source = (
        (tile_src[None, :] == jnp.arange(source_count, dtype=jnp.int32)[:, None]) & usable[None, :]
    ).astype(jnp.float32)
    products = jnp.einsum(
        "tij,tjf->tif", tile_vals, source[tile_src], preferred_element_type=jnp.float32
    )
    summed = jnp.einsum("bt,tif->bif", to_target, products, precision=lax.Precision.HIGHEST)
    unit_column = jnp.ones((tile_size,), jnp.bfloat16)
    row_sums = jnp.einsum("tij,j->ti", tile_vals, unit_column, preferred_element_type=jnp.float32)
    degree = jnp.dot(to_target, row_sums, precision=lax.Precision.HIGHEST)
    agg = (summed / degree[:, :, None]).reshape(node_count, width).astype(jnp.bfloat16)
    preact = jnp.dot(features, w_self, preferred_element_type=jnp.float32) + jnp.dot(
        agg, w_neigh, preferred_element_type=jnp.float32
    )
    sigm = jax.nn.sigmoid(preact)
    output = (preact * sigm).astype(jnp.bfloat16)
    grad_pre = (cotangent.astype(jnp.float32) * sigm * (1.0 + preact * (1.0 - sigm))).astype(
        jnp.bfloat16
    )
    part_self = jnp.einsum("nf,nh->fh", features, grad_pre, preferred_element_type=jnp.float32)
    part_neigh = jnp.einsum("nf,nh->fh", agg, grad_pre, preferred_element_type=jnp.float32)
    grad_own = jnp.einsum("nh,fh->nf", grad_pre, w_self, preferred_element_type=jnp.float32)
    grad_agg = jnp.einsum("nh,fh->nf", grad_pre, w_neigh, preferred_element_type=jnp.float32)
    grad_agg = (grad_agg / degree.reshape(-1)[:, None]).astype(jnp.bfloat16)
    picked = grad_agg.reshape(block_count, tile_size, width)[tile_tgt]
    backward = jnp.einsum("tij,tif->tjf", tile_vals, picked, preferred_element_type=jnp.float32)
    grad_source = jnp.einsum(
        "st,tjf->sjf", to_source, backward, precision=lax.Precision.HIGHEST
    ).reshape(-1, width)
    dom_rows = dom_peers * dom_index.shape[1]
    back_dom = (
        grad_source[node_count : node_count + dom_rows]
        .reshape(dom_index.shape[0], dom_index.shape[1], width)
        .astype(jnp.bfloat16)
    )
    back_grp = (
        grad_source[node_count + dom_rows :]
        .reshape(grp_index.shape[0], grp_index.shape[1], width)
        .astype(jnp.bfloat16)
    )
    ret_dom = lax.all_to_all(back_dom, "dom", split_axis=0, concat_axis=0, tiled=True)
    ret_grp = lax.all_to_all(back_grp, "grp", split_axis=0, concat_axis=0, tiled=True)
    grad_self, grad_neigh = weight_sum(part_self, part_neigh)
    grad_total = grad_own + grad_source[:node_count]
    grad_total = grad_total.at[dom_index.reshape(-1)].add(
        ret_dom.reshape(-1, width).astype(jnp.float32)
    )
    grad_total = grad_total.at[grp_index.reshape(-1)].add(
        ret_grp.reshape(-1, width).astype(jnp.float32)
    )
    return (output, grad_total.astype(jnp.bfloat16), grad_self, grad_neigh)


def solution(mesh):
    return jax.shard_map(
        per_device,
        mesh=mesh,
        in_specs=(
            P(("dom", "grp"), None),
            P(("dom", "grp"), None, None),
            P(("dom", "grp"), None, None),
            P(("dom", "grp"), None, None),
            P(("dom", "grp")),
            P(("dom", "grp")),
            P(("dom", "grp")),
            P(),
            P(),
            P(("dom", "grp"), None),
        ),
        out_specs=(P(("dom", "grp"), None), P(("dom", "grp"), None), P(), P()),
        check_vma=False,
    )
```

```python
import jax
import jax.numpy as jnp
from jax import lax
from jax.sharding import PartitionSpec as P


def weight_sum(part_self, part_neigh):
    axes = ("dom", "grp")
    peers = lax.psum(1, axes)
    rows = part_self.shape[0]
    stacked = jnp.concatenate([part_self, part_neigh], axis=0)
    flat = stacked.reshape(-1)
    pad = (-flat.shape[0]) % peers
    chunks = jnp.pad(flat, (0, pad)).reshape(peers, -1)
    mine = jnp.sum(lax.all_to_all(chunks, axes, 0, 0, tiled=True), axis=0, keepdims=True)
    spread = jnp.broadcast_to(mine, chunks.shape)
    total = lax.all_to_all(spread, axes, 0, 0, tiled=True).reshape(-1)
    total = total[: flat.shape[0]].reshape(stacked.shape)
    return total[:rows], total[rows:]


def exchange(dom_part, grp_part):
    axes = ("dom", "grp")
    n_dom, n_grp = dom_part.shape[0], grp_part.shape[0]
    a = lax.axis_index("dom")
    b = lax.axis_index("grp")
    cell = dom_part.shape[1:]
    buf = jnp.zeros((n_dom, n_grp) + cell, dom_part.dtype)
    buf = lax.dynamic_update_slice_in_dim(buf, dom_part[:, None], b, axis=1)
    buf = lax.dynamic_update_slice_in_dim(buf, grp_part[None], a, axis=0)
    got = lax.all_to_all(buf.reshape((n_dom * n_grp,) + cell), axes, 0, 0, tiled=True)
    got = got.reshape((n_dom, n_grp) + cell)
    from_dom = lax.dynamic_index_in_dim(got, b, axis=1, keepdims=False)
    own_dom = lax.dynamic_index_in_dim(dom_part, a, axis=0, keepdims=True)
    from_dom = lax.dynamic_update_slice_in_dim(from_dom, own_dom, a, axis=0)
    from_grp = lax.dynamic_index_in_dim(got, a, axis=0, keepdims=False)
    return from_dom, from_grp


def one_hot_rows(index, count):
    return (index.reshape(-1)[:, None] == jnp.arange(count, dtype=jnp.int32)[None, :]).astype(jnp.bfloat16)


def per_device(
    features,
    send_dom,
    send_grp,
    tile_vals,
    tile_tgt,
    tile_src,
    tile_count,
    w_self,
    w_neigh,
    cotangent,
):
    tile_size = tile_vals.shape[1]
    width = features.shape[1]
    node_count = features.shape[0]
    block_count = node_count // tile_size
    dom_index = send_dom[0]
    grp_index = send_grp[0]
    n_dom, bnd = dom_index.shape
    n_grp = grp_index.shape[0]
    send_index = jnp.concatenate([dom_index.reshape(-1), grp_index.reshape(-1)])
    pick = one_hot_rows(send_index, node_count)
    sent = jnp.dot(pick, features, preferred_element_type=jnp.float32).astype(jnp.bfloat16)
    sent = sent.reshape(n_dom + n_grp, bnd, width)
    recv_dom, recv_grp = exchange(sent[:n_dom], sent[n_dom:])
    source = jnp.concatenate(
        [features, recv_dom.reshape(-1, width), recv_grp.reshape(-1, width)], axis=0
    )
    source = source.reshape(-1, tile_size, width)
    source_count = source.shape[0]
    slot_count = tile_vals.shape[0]
    usable = jnp.arange(slot_count, dtype=jnp.int32) < tile_count[0]
    to_target = (
        (tile_tgt[None, :] == jnp.arange(block_count, dtype=jnp.int32)[:, None]) & usable[None, :]
    ).astype(jnp.float32)
    to_source = (
        (tile_src[None, :] == jnp.arange(source_count, dtype=jnp.int32)[:, None]) & usable[None, :]
    ).astype(jnp.float32)
    products = jnp.einsum(
        "tij,tjf->tif", tile_vals, source[tile_src], preferred_element_type=jnp.float32
    )
    summed = jnp.einsum("bt,tif->bif", to_target, products, precision=lax.Precision.HIGHEST)
    unit_column = jnp.ones((tile_size,), jnp.bfloat16)
    row_sums = jnp.einsum("tij,j->ti", tile_vals, unit_column, preferred_element_type=jnp.float32)
    degree = jnp.dot(to_target, row_sums, precision=lax.Precision.HIGHEST)
    agg = (summed / degree[:, :, None]).reshape(node_count, width).astype(jnp.bfloat16)
    preact = jnp.dot(features, w_self, preferred_element_type=jnp.float32) + jnp.dot(
        agg, w_neigh, preferred_element_type=jnp.float32
    )
    sigm = jax.nn.sigmoid(preact)
    output = (preact * sigm).astype(jnp.bfloat16)
    grad_pre = (cotangent.astype(jnp.float32) * sigm * (1.0 + preact * (1.0 - sigm))).astype(
        jnp.bfloat16
    )
    part_self = jnp.einsum("nf,nh->fh", features, grad_pre, preferred_element_type=jnp.float32)
    part_neigh = jnp.einsum("nf,nh->fh", agg, grad_pre, preferred_element_type=jnp.float32)
    grad_own = jnp.einsum("nh,fh->nf", grad_pre, w_self, preferred_element_type=jnp.float32)
    grad_agg = jnp.einsum("nh,fh->nf", grad_pre, w_neigh, preferred_element_type=jnp.float32)
    grad_agg = (grad_agg / degree.reshape(-1)[:, None]).astype(jnp.bfloat16)
    picked = grad_agg.reshape(block_count, tile_size, width)[tile_tgt]
    backward = jnp.einsum("tij,tif->tjf", tile_vals, picked, preferred_element_type=jnp.float32)
    grad_source = jnp.einsum(
        "st,tjf->sjf", to_source, backward, precision=lax.Precision.HIGHEST
    ).reshape(-1, width)
    remote = grad_source[node_count:].astype(jnp.bfloat16).reshape(n_dom + n_grp, bnd, width)
    ret_dom, ret_grp = exchange(remote[:n_dom], remote[n_dom:])
    grad_self, grad_neigh = weight_sum(part_self, part_neigh)
    returned = jnp.concatenate([ret_dom.reshape(-1, width), ret_grp.reshape(-1, width)])
    grad_total = grad_own + grad_source[:node_count]
    grad_total = grad_total + lax.dot_general(
        pick, returned, (((0,), (0,)), ((), ())), preferred_element_type=jnp.float32
    )
    return (output, grad_total.astype(jnp.bfloat16), grad_self, grad_neigh)


def solution(mesh):
    return jax.shard_map(
        per_device,
        mesh=mesh,
        in_specs=(
            P(("dom", "grp"), None),
            P(("dom", "grp"), None, None),
            P(("dom", "grp"), None, None),
            P(("dom", "grp"), None, None),
            P(("dom", "grp")),
            P(("dom", "grp")),
            P(("dom", "grp")),
            P(),
            P(),
            P(("dom", "grp"), None),
        ),
        out_specs=(P(("dom", "grp"), None), P(("dom", "grp"), None), P(), P()),
        check_vma=False,
    )
```

```python
import jax
import jax.numpy as jnp
from jax import lax
from jax.sharding import PartitionSpec as P
from jax.experimental import pallas as pl
from jax.experimental.pallas import tpu as pltpu


def weight_sum(part_self, part_neigh):
    axes = ("dom", "grp")
    peers = lax.psum(1, axes)
    rows = part_self.shape[0]
    stacked = jnp.concatenate([part_self, part_neigh], axis=0)
    flat = stacked.reshape(-1)
    pad = (-flat.shape[0]) % peers
    chunks = jnp.pad(flat, (0, pad)).reshape(peers, -1)
    mine = jnp.sum(lax.all_to_all(chunks, axes, 0, 0, tiled=True), axis=0, keepdims=True)
    spread = jnp.broadcast_to(mine, chunks.shape)
    total = lax.all_to_all(spread, axes, 0, 0, tiled=True).reshape(-1)
    total = total[: flat.shape[0]].reshape(stacked.shape)
    return total[:rows], total[rows:]


def exchange(dom_part, grp_part):
    axes = ("dom", "grp")
    n_dom, n_grp = dom_part.shape[0], grp_part.shape[0]
    a = lax.axis_index("dom")
    b = lax.axis_index("grp")
    cell = dom_part.shape[1:]
    buf = jnp.zeros((n_dom, n_grp) + cell, dom_part.dtype)
    buf = lax.dynamic_update_slice_in_dim(buf, dom_part[:, None], b, axis=1)
    buf = lax.dynamic_update_slice_in_dim(buf, grp_part[None], a, axis=0)
    got = lax.all_to_all(buf.reshape((n_dom * n_grp,) + cell), axes, 0, 0, tiled=True)
    got = got.reshape((n_dom, n_grp) + cell)
    from_dom = lax.dynamic_index_in_dim(got, b, axis=1, keepdims=False)
    own_dom = lax.dynamic_index_in_dim(dom_part, a, axis=0, keepdims=True)
    from_dom = lax.dynamic_update_slice_in_dim(from_dom, own_dom, a, axis=0)
    from_grp = lax.dynamic_index_in_dim(got, a, axis=0, keepdims=False)
    return from_dom, from_grp


def one_hot_rows(index, count):
    return (index.reshape(-1)[:, None] == jnp.arange(count, dtype=jnp.int32)[None, :]).astype(jnp.bfloat16)


def tile_pass(tile_tgt, tile_src, tile_count, tile_vals, blocks, out_count, transpose):
    slots, size, _ = tile_vals.shape
    in_count, _, wide = blocks.shape

    def kernel(tgt_ref, src_ref, cnt_ref, tiles_ref, blocks_ref, out_ref):
        out_ref[...] = jnp.zeros_like(out_ref)

        def body(t, carry):
            @pl.when(t < cnt_ref[0])
            def _():
                if transpose:
                    read, write = tgt_ref[t], src_ref[t]
                    part = lax.dot_general(
                        tiles_ref[t], blocks_ref[read], (((0,), (0,)), ((), ())),
                        preferred_element_type=jnp.float32,
                    )
                else:
                    read, write = src_ref[t], tgt_ref[t]
                    part = jnp.dot(tiles_ref[t], blocks_ref[read], preferred_element_type=jnp.float32)
                out_ref[write] += part

            return carry

        lax.fori_loop(0, slots, body, 0)

    whole = lambda i, *_: (0, 0, 0)
    return pl.pallas_call(
        kernel,
        grid_spec=pltpu.PrefetchScalarGridSpec(
            num_scalar_prefetch=3,
            grid=(1,),
            in_specs=[
                pl.BlockSpec((slots, size, size), whole),
                pl.BlockSpec((in_count, size, wide), whole),
            ],
            out_specs=pl.BlockSpec((out_count, size, wide), whole),
        ),
        out_shape=jax.ShapeDtypeStruct((out_count, size, wide), jnp.float32),
    )(tile_tgt, tile_src, tile_count, tile_vals, blocks)


def per_device(
    features,
    send_dom,
    send_grp,
    tile_vals,
    tile_tgt,
    tile_src,
    tile_count,
    w_self,
    w_neigh,
    cotangent,
):
    tile_size = tile_vals.shape[1]
    width = features.shape[1]
    node_count = features.shape[0]
    block_count = node_count // tile_size
    dom_index = send_dom[0]
    grp_index = send_grp[0]
    n_dom, bnd = dom_index.shape
    n_grp = grp_index.shape[0]
    send_index = jnp.concatenate([dom_index.reshape(-1), grp_index.reshape(-1)])
    pick = one_hot_rows(send_index, node_count)
    sent = jnp.dot(pick, features, preferred_element_type=jnp.float32).astype(jnp.bfloat16)
    sent = sent.reshape(n_dom + n_grp, bnd, width)
    recv_dom, recv_grp = exchange(sent[:n_dom], sent[n_dom:])
    source = jnp.concatenate(
        [features, recv_dom.reshape(-1, width), recv_grp.reshape(-1, width)], axis=0
    )
    source = source.reshape(-1, tile_size, width)
    source_count = source.shape[0]
    ones = jnp.ones(source.shape[:2] + (width,), source.dtype)
    acc = tile_pass(
        tile_tgt, tile_src, tile_count, tile_vals, jnp.concatenate([source, ones], axis=2),
        block_count, False,
    )
    degree = acc[:, :, width]
    agg = (acc[:, :, :width] / degree[:, :, None]).reshape(node_count, width).astype(jnp.bfloat16)
    preact = jnp.dot(features, w_self, preferred_element_type=jnp.float32) + jnp.dot(
        agg, w_neigh, preferred_element_type=jnp.float32
    )
    sigm = jax.nn.sigmoid(preact)
    output = (preact * sigm).astype(jnp.bfloat16)
    grad_pre = (cotangent.astype(jnp.float32) * sigm * (1.0 + preact * (1.0 - sigm))).astype(
        jnp.bfloat16
    )
    part_self = jnp.einsum("nf,nh->fh", features, grad_pre, preferred_element_type=jnp.float32)
    part_neigh = jnp.einsum("nf,nh->fh", agg, grad_pre, preferred_element_type=jnp.float32)
    grad_own = jnp.einsum("nh,fh->nf", grad_pre, w_self, preferred_element_type=jnp.float32)
    grad_agg = jnp.einsum("nh,fh->nf", grad_pre, w_neigh, preferred_element_type=jnp.float32)
    grad_agg = (grad_agg / degree.reshape(-1)[:, None]).astype(jnp.bfloat16)
    grad_source = tile_pass(
        tile_tgt, tile_src, tile_count, tile_vals, grad_agg.reshape(block_count, tile_size, width),
        source_count, True,
    ).reshape(-1, width)
    remote = grad_source[node_count:].astype(jnp.bfloat16).reshape(n_dom + n_grp, bnd, width)
    ret_dom, ret_grp = exchange(remote[:n_dom], remote[n_dom:])
    grad_self, grad_neigh = weight_sum(part_self, part_neigh)
    returned = jnp.concatenate([ret_dom.reshape(-1, width), ret_grp.reshape(-1, width)])
    grad_total = grad_own + grad_source[:node_count]
    grad_total = grad_total + lax.dot_general(
        pick, returned, (((0,), (0,)), ((), ())), preferred_element_type=jnp.float32
    )
    return (output, grad_total.astype(jnp.bfloat16), grad_self, grad_neigh)


def solution(mesh):
    return jax.shard_map(
        per_device,
        mesh=mesh,
        in_specs=(
            P(("dom", "grp"), None),
            P(("dom", "grp"), None, None),
            P(("dom", "grp"), None, None),
            P(("dom", "grp"), None, None),
            P(("dom", "grp")),
            P(("dom", "grp")),
            P(("dom", "grp")),
            P(),
            P(),
            P(("dom", "grp"), None),
        ),
        out_specs=(P(("dom", "grp"), None), P(("dom", "grp"), None), P(), P()),
        check_vma=False,
    )
```

```python
import jax
import jax.numpy as jnp
from jax import lax
from jax.sharding import PartitionSpec as P
from jax.experimental import pallas as pl
from jax.experimental.pallas import tpu as pltpu


MERGE_LIMIT = 4 << 20


def weight_chunks(part_self, part_neigh, peers):
    flat = jnp.concatenate([part_self, part_neigh], axis=0).reshape(-1)
    pad = (-flat.shape[0]) % peers
    return jnp.pad(flat, (0, pad)).reshape(peers, -1)


def weight_spread(received, part_self, part_neigh):
    axes = ("dom", "grp")
    rows = part_self.shape[0]
    mine = jnp.sum(received, axis=0, keepdims=True)
    spread = jnp.broadcast_to(mine, received.shape)
    total = lax.all_to_all(spread, axes, 0, 0, tiled=True).reshape(-1)
    total = total[: 2 * part_self.size].reshape(2 * rows, -1)
    return total[:rows], total[rows:]


def exchange(dom_part, grp_part, extra=None):
    axes = ("dom", "grp")
    n_dom, n_grp = dom_part.shape[0], grp_part.shape[0]
    a = lax.axis_index("dom")
    b = lax.axis_index("grp")
    cell = dom_part.shape[1:]
    buf = jnp.zeros((n_dom, n_grp) + cell, dom_part.dtype)
    buf = lax.dynamic_update_slice_in_dim(buf, dom_part[:, None], b, axis=1)
    buf = lax.dynamic_update_slice_in_dim(buf, grp_part[None], a, axis=0)
    if extra is not None:
        extra = extra.reshape((n_dom, n_grp, -1) + cell[1:]).astype(buf.dtype)
        buf = jnp.concatenate([buf, extra], axis=2)
    got = lax.all_to_all(buf.reshape((n_dom * n_grp,) + buf.shape[2:]), axes, 0, 0, tiled=True)
    got = got.reshape((n_dom, n_grp) + buf.shape[2:])
    rows = got[:, :, : cell[0]]
    from_dom = lax.dynamic_index_in_dim(rows, b, axis=1, keepdims=False)
    own_dom = lax.dynamic_index_in_dim(dom_part, a, axis=0, keepdims=True)
    from_dom = lax.dynamic_update_slice_in_dim(from_dom, own_dom, a, axis=0)
    from_grp = lax.dynamic_index_in_dim(rows, a, axis=0, keepdims=False)
    if extra is None:
        return from_dom, from_grp
    return from_dom, from_grp, got[:, :, cell[0] :].reshape(n_dom * n_grp, -1)


def one_hot_rows(index, count):
    return (index.reshape(-1)[:, None] == jnp.arange(count, dtype=jnp.int32)[None, :]).astype(jnp.bfloat16)


def tile_pass(tile_tgt, tile_src, tile_count, tile_vals, blocks, out_count, transpose):
    slots, size, _ = tile_vals.shape
    in_count, _, wide = blocks.shape

    def kernel(tgt_ref, src_ref, cnt_ref, tiles_ref, blocks_ref, out_ref):
        out_ref[...] = jnp.zeros_like(out_ref)

        def body(t, carry):
            @pl.when(t < cnt_ref[0])
            def _():
                if transpose:
                    read, write = tgt_ref[t], src_ref[t]
                    part = lax.dot_general(
                        tiles_ref[t], blocks_ref[read], (((0,), (0,)), ((), ())),
                        preferred_element_type=jnp.float32,
                    )
                else:
                    read, write = src_ref[t], tgt_ref[t]
                    part = jnp.dot(tiles_ref[t], blocks_ref[read], preferred_element_type=jnp.float32)
                out_ref[write] += part

            return carry

        lax.fori_loop(0, slots, body, 0)

    whole = lambda i, *_: (0, 0, 0)
    return pl.pallas_call(
        kernel,
        grid_spec=pltpu.PrefetchScalarGridSpec(
            num_scalar_prefetch=3,
            grid=(1,),
            in_specs=[
                pl.BlockSpec((slots, size, size), whole),
                pl.BlockSpec((in_count, size, wide), whole),
            ],
            out_specs=pl.BlockSpec((out_count, size, wide), whole),
        ),
        out_shape=jax.ShapeDtypeStruct((out_count, size, wide), jnp.float32),
    )(tile_tgt, tile_src, tile_count, tile_vals, blocks)


def per_device(
    features,
    send_dom,
    send_grp,
    tile_vals,
    tile_tgt,
    tile_src,
    tile_count,
    w_self,
    w_neigh,
    cotangent,
):
    tile_size = tile_vals.shape[1]
    width = features.shape[1]
    node_count = features.shape[0]
    block_count = node_count // tile_size
    dom_index = send_dom[0]
    grp_index = send_grp[0]
    n_dom, bnd = dom_index.shape
    n_grp = grp_index.shape[0]
    send_index = jnp.concatenate([dom_index.reshape(-1), grp_index.reshape(-1)])
    pick = one_hot_rows(send_index, node_count)
    sent = jnp.dot(pick, features, preferred_element_type=jnp.float32).astype(jnp.bfloat16)
    sent = sent.reshape(n_dom + n_grp, bnd, width)
    recv_dom, recv_grp = exchange(sent[:n_dom], sent[n_dom:])
    source = jnp.concatenate(
        [features, recv_dom.reshape(-1, width), recv_grp.reshape(-1, width)], axis=0
    )
    source = source.reshape(-1, tile_size, width)
    source_count = source.shape[0]
    ones = jnp.ones(source.shape[:2] + (width,), source.dtype)
    acc = tile_pass(
        tile_tgt, tile_src, tile_count, tile_vals, jnp.concatenate([source, ones], axis=2),
        block_count, False,
    )
    degree = acc[:, :, width]
    agg = (acc[:, :, :width] / degree[:, :, None]).reshape(node_count, width).astype(jnp.bfloat16)
    preact = jnp.dot(features, w_self, preferred_element_type=jnp.float32) + jnp.dot(
        agg, w_neigh, preferred_element_type=jnp.float32
    )
    sigm = jax.nn.sigmoid(preact)
    output = (preact * sigm).astype(jnp.bfloat16)
    grad_pre = (cotangent.astype(jnp.float32) * sigm * (1.0 + preact * (1.0 - sigm))).astype(
        jnp.bfloat16
    )
    part_self = jnp.einsum("nf,nh->fh", features, grad_pre, preferred_element_type=jnp.float32)
    part_neigh = jnp.einsum("nf,nh->fh", agg, grad_pre, preferred_element_type=jnp.float32)
    grad_own = jnp.einsum("nh,fh->nf", grad_pre, w_self, preferred_element_type=jnp.float32)
    grad_agg = jnp.einsum("nh,fh->nf", grad_pre, w_neigh, preferred_element_type=jnp.float32)
    grad_agg = (grad_agg / degree.reshape(-1)[:, None]).astype(jnp.bfloat16)
    grad_source = tile_pass(
        tile_tgt, tile_src, tile_count, tile_vals, grad_agg.reshape(block_count, tile_size, width),
        source_count, True,
    ).reshape(-1, width)
    remote = grad_source[node_count:].astype(jnp.bfloat16).reshape(n_dom + n_grp, bnd, width)
    peers = n_dom * n_grp
    chunks = weight_chunks(part_self, part_neigh, peers)
    merged_bytes = peers * (bnd * width + chunks.shape[1]) * 4
    if merged_bytes <= MERGE_LIMIT and chunks.shape[1] % width == 0:
        ret_dom, ret_grp, received = exchange(
            remote[:n_dom].astype(jnp.float32), remote[n_dom:].astype(jnp.float32), chunks
        )
    else:
        ret_dom, ret_grp = exchange(remote[:n_dom], remote[n_dom:])
        received = lax.all_to_all(chunks, ("dom", "grp"), 0, 0, tiled=True)
    grad_self, grad_neigh = weight_spread(received, part_self, part_neigh)
    returned = jnp.concatenate([ret_dom.reshape(-1, width), ret_grp.reshape(-1, width)])
    returned = returned.astype(jnp.bfloat16)
    grad_total = grad_own + grad_source[:node_count]
    grad_total = grad_total + lax.dot_general(
        pick, returned, (((0,), (0,)), ((), ())), preferred_element_type=jnp.float32
    )
    return (output, grad_total.astype(jnp.bfloat16), grad_self, grad_neigh)


def solution(mesh):
    return jax.shard_map(
        per_device,
        mesh=mesh,
        in_specs=(
            P(("dom", "grp"), None),
            P(("dom", "grp"), None, None),
            P(("dom", "grp"), None, None),
            P(("dom", "grp"), None, None),
            P(("dom", "grp")),
            P(("dom", "grp")),
            P(("dom", "grp")),
            P(),
            P(),
            P(("dom", "grp"), None),
        ),
        out_specs=(P(("dom", "grp"), None), P(("dom", "grp"), None), P(), P()),
        check_vma=False,
    )
```

```python
import jax
import jax.numpy as jnp
from jax import lax
from jax.sharding import PartitionSpec as P
from jax.experimental import pallas as pl
from jax.experimental.pallas import tpu as pltpu


def weight_sum(part_self, part_neigh):
    axes = ("dom", "grp")
    peers = lax.psum(1, axes)
    rows = part_self.shape[0]
    stacked = jnp.concatenate([part_self, part_neigh], axis=0)
    flat = stacked.reshape(-1)
    pad = (-flat.shape[0]) % peers
    chunks = jnp.pad(flat, (0, pad)).reshape(peers, -1)
    mine = jnp.sum(lax.all_to_all(chunks, axes, 0, 0, tiled=True), axis=0, keepdims=True)
    spread = jnp.broadcast_to(mine, chunks.shape)
    total = lax.all_to_all(spread, axes, 0, 0, tiled=True).reshape(-1)
    total = total[: flat.shape[0]].reshape(stacked.shape)
    return total[:rows], total[rows:]


def exchange(dom_part, grp_part):
    axes = ("dom", "grp")
    n_dom, n_grp = dom_part.shape[0], grp_part.shape[0]
    a = lax.axis_index("dom")
    b = lax.axis_index("grp")
    cell = dom_part.shape[1:]
    buf = jnp.zeros((n_dom, n_grp) + cell, dom_part.dtype)
    buf = lax.dynamic_update_slice_in_dim(buf, dom_part[:, None], b, axis=1)
    buf = lax.dynamic_update_slice_in_dim(buf, grp_part[None], a, axis=0)
    got = lax.all_to_all(buf.reshape((n_dom * n_grp,) + cell), axes, 0, 0, tiled=True)
    got = got.reshape((n_dom, n_grp) + cell)
    from_dom = lax.dynamic_index_in_dim(got, b, axis=1, keepdims=False)
    own_dom = lax.dynamic_index_in_dim(dom_part, a, axis=0, keepdims=True)
    from_dom = lax.dynamic_update_slice_in_dim(from_dom, own_dom, a, axis=0)
    from_grp = lax.dynamic_index_in_dim(got, a, axis=0, keepdims=False)
    return from_dom, from_grp


def one_hot_rows(index, count):
    return (index.reshape(-1)[:, None] == jnp.arange(count, dtype=jnp.int32)[None, :]).astype(jnp.bfloat16)


def tile_pass(tile_tgt, tile_src, tile_count, tile_vals, blocks, out_count, transpose, first=0, init=None):
    slots, size, _ = tile_vals.shape
    in_count, _, wide = blocks.shape

    def kernel(tgt_ref, src_ref, cnt_ref, tiles_ref, blocks_ref, *rest):
        if init is None:
            (out_ref,) = rest
            out_ref[...] = jnp.zeros_like(out_ref)
        else:
            init_ref, out_ref = rest
            out_ref[...] = init_ref[...]

        def body(t, carry):
            if transpose:
                live = t < cnt_ref[0]
            else:
                block = src_ref[t] - first
                live = (t < cnt_ref[0]) & (block >= 0) & (block < in_count)

            @pl.when(live)
            def _():
                if transpose:
                    read, write = tgt_ref[t], src_ref[t]
                    part = lax.dot_general(
                        tiles_ref[t], blocks_ref[read], (((0,), (0,)), ((), ())),
                        preferred_element_type=jnp.float32,
                    )
                else:
                    read, write = src_ref[t] - first, tgt_ref[t]
                    part = jnp.dot(tiles_ref[t], blocks_ref[read], preferred_element_type=jnp.float32)
                out_ref[write] += part

            return carry

        lax.fori_loop(0, slots, body, 0)

    whole = lambda i, *_: (0, 0, 0)
    in_specs = [
        pl.BlockSpec((slots, size, size), whole),
        pl.BlockSpec((in_count, size, wide), whole),
    ]
    operands = [tile_tgt, tile_src, tile_count, tile_vals, blocks]
    if init is not None:
        in_specs.append(pl.BlockSpec((out_count, size, wide), whole))
        operands.append(init)
    return pl.pallas_call(
        kernel,
        grid_spec=pltpu.PrefetchScalarGridSpec(
            num_scalar_prefetch=3,
            grid=(1,),
            in_specs=in_specs,
            out_specs=pl.BlockSpec((out_count, size, wide), whole),
        ),
        out_shape=jax.ShapeDtypeStruct((out_count, size, wide), jnp.float32),
    )(*operands)


def per_device(
    features,
    send_dom,
    send_grp,
    tile_vals,
    tile_tgt,
    tile_src,
    tile_count,
    w_self,
    w_neigh,
    cotangent,
):
    tile_size = tile_vals.shape[1]
    width = features.shape[1]
    node_count = features.shape[0]
    block_count = node_count // tile_size
    dom_index = send_dom[0]
    grp_index = send_grp[0]
    n_dom, bnd = dom_index.shape
    n_grp = grp_index.shape[0]
    send_index = jnp.concatenate([dom_index.reshape(-1), grp_index.reshape(-1)])
    pick = one_hot_rows(send_index, node_count)
    sent = jnp.dot(pick, features, preferred_element_type=jnp.float32).astype(jnp.bfloat16)
    sent = sent.reshape(n_dom + n_grp, bnd, width)
    with_ones = lambda rows: jnp.concatenate(
        [rows, jnp.ones(rows.shape, rows.dtype)], axis=1
    ).reshape(-1, tile_size, 2 * width)
    acc_own = tile_pass(
        tile_tgt, tile_src, tile_count, tile_vals, with_ones(features), block_count, False
    )
    recv_dom, recv_grp = exchange(sent[:n_dom], sent[n_dom:])
    received = jnp.concatenate([recv_dom.reshape(-1, width), recv_grp.reshape(-1, width)], axis=0)
    source_count = block_count + received.shape[0] // tile_size
    acc = tile_pass(
        tile_tgt, tile_src, tile_count, tile_vals, with_ones(received), block_count, False,
        first=block_count, init=acc_own,
    )
    degree = acc[:, :, width]
    agg = (acc[:, :, :width] / degree[:, :, None]).reshape(node_count, width).astype(jnp.bfloat16)
    preact = jnp.dot(features, w_self, preferred_element_type=jnp.float32) + jnp.dot(
        agg, w_neigh, preferred_element_type=jnp.float32
    )
    sigm = jax.nn.sigmoid(preact)
    output = (preact * sigm).astype(jnp.bfloat16)
    grad_pre = (cotangent.astype(jnp.float32) * sigm * (1.0 + preact * (1.0 - sigm))).astype(
        jnp.bfloat16
    )
    part_self = jnp.einsum("nf,nh->fh", features, grad_pre, preferred_element_type=jnp.float32)
    part_neigh = jnp.einsum("nf,nh->fh", agg, grad_pre, preferred_element_type=jnp.float32)
    grad_own = jnp.einsum("nh,fh->nf", grad_pre, w_self, preferred_element_type=jnp.float32)
    grad_agg = jnp.einsum("nh,fh->nf", grad_pre, w_neigh, preferred_element_type=jnp.float32)
    grad_agg = (grad_agg / degree.reshape(-1)[:, None]).astype(jnp.bfloat16)
    grad_source = tile_pass(
        tile_tgt, tile_src, tile_count, tile_vals, grad_agg.reshape(block_count, tile_size, width),
        source_count, True,
    ).reshape(-1, width)
    remote = grad_source[node_count:].astype(jnp.bfloat16).reshape(n_dom + n_grp, bnd, width)
    ret_dom, ret_grp = exchange(remote[:n_dom], remote[n_dom:])
    grad_self, grad_neigh = weight_sum(part_self, part_neigh)
    returned = jnp.concatenate([ret_dom.reshape(-1, width), ret_grp.reshape(-1, width)])
    grad_total = grad_own + grad_source[:node_count]
    grad_total = grad_total + lax.dot_general(
        pick, returned, (((0,), (0,)), ((), ())), preferred_element_type=jnp.float32
    )
    return (output, grad_total.astype(jnp.bfloat16), grad_self, grad_neigh)


def solution(mesh):
    return jax.shard_map(
        per_device,
        mesh=mesh,
        in_specs=(
            P(("dom", "grp"), None),
            P(("dom", "grp"), None, None),
            P(("dom", "grp"), None, None),
            P(("dom", "grp"), None, None),
            P(("dom", "grp")),
            P(("dom", "grp")),
            P(("dom", "grp")),
            P(),
            P(),
            P(("dom", "grp"), None),
        ),
        out_specs=(P(("dom", "grp"), None), P(("dom", "grp"), None), P(), P()),
        check_vma=False,
    )
```

```python
import jax
import jax.numpy as jnp
from jax import lax
from jax.sharding import PartitionSpec as P
from jax.experimental import pallas as pl
from jax.experimental.pallas import tpu as pltpu


def weight_sum(part_self, part_neigh):
    axes = ("dom", "grp")
    peers = lax.psum(1, axes)
    rows = part_self.shape[0]
    stacked = jnp.concatenate([part_self, part_neigh], axis=0)
    flat = stacked.reshape(-1)
    pad = (-flat.shape[0]) % peers
    chunks = jnp.pad(flat, (0, pad)).reshape(peers, -1)
    mine = jnp.sum(lax.all_to_all(chunks, axes, 0, 0, tiled=True), axis=0, keepdims=True)
    spread = jnp.broadcast_to(mine, chunks.shape)
    total = lax.all_to_all(spread, axes, 0, 0, tiled=True).reshape(-1)
    total = total[: flat.shape[0]].reshape(stacked.shape)
    return total[:rows], total[rows:]


def exchange(dom_part, grp_part):
    axes = ("dom", "grp")
    n_dom, n_grp = dom_part.shape[0], grp_part.shape[0]
    a = lax.axis_index("dom")
    b = lax.axis_index("grp")
    cell = dom_part.shape[1:]
    buf = jnp.zeros((n_dom, n_grp) + cell, dom_part.dtype)
    buf = lax.dynamic_update_slice_in_dim(buf, dom_part[:, None], b, axis=1)
    buf = lax.dynamic_update_slice_in_dim(buf, grp_part[None], a, axis=0)
    got = lax.all_to_all(buf.reshape((n_dom * n_grp,) + cell), axes, 0, 0, tiled=True)
    got = got.reshape((n_dom, n_grp) + cell)
    from_dom = lax.dynamic_index_in_dim(got, b, axis=1, keepdims=False)
    own_dom = lax.dynamic_index_in_dim(dom_part, a, axis=0, keepdims=True)
    from_dom = lax.dynamic_update_slice_in_dim(from_dom, own_dom, a, axis=0)
    from_grp = lax.dynamic_index_in_dim(got, a, axis=0, keepdims=False)
    return from_dom, from_grp


def one_hot_rows(index, count):
    return (index.reshape(-1)[:, None] == jnp.arange(count, dtype=jnp.int32)[None, :]).astype(jnp.bfloat16)


def tile_pass(tile_tgt, tile_src, tile_count, tile_vals, blocks, out_count, transpose, first=0, init=None):
    slots, size, _ = tile_vals.shape
    in_count, _, wide = blocks.shape
    with_degree = not transpose and init is None

    def kernel(tgt_ref, src_ref, cnt_ref, tiles_hbm, blocks_ref, *rest):
        rest = list(rest)
        init_ref = rest.pop(0) if init is not None else None
        out_ref = rest.pop(0)
        deg_ref = rest.pop(0) if with_degree else None
        tiles_buf, sems = rest
        if init is None:
            out_ref[...] = jnp.zeros_like(out_ref)
        else:
            out_ref[...] = init_ref[...]
        if with_degree:
            deg_ref[...] = jnp.zeros_like(deg_ref)

        def live(t):
            alive = t < cnt_ref[0]
            if transpose or with_degree:
                return alive
            block = src_ref[t] - first
            return alive & (block >= 0) & (block < in_count)

        def copy(t):
            return pltpu.make_async_copy(tiles_hbm.at[t], tiles_buf.at[t], sems.at[t])

        def issue(t, carry):
            @pl.when(live(t))
            def _():
                copy(t).start()

            return carry

        lax.fori_loop(0, slots, issue, 0)

        def body(t, carry):
            @pl.when(live(t))
            def _():
                copy(t).wait()
                tile = tiles_buf[t]
                if transpose:
                    part = lax.dot_general(
                        tile, blocks_ref[tgt_ref[t]], (((0,), (0,)), ((), ())),
                        preferred_element_type=jnp.float32,
                    )
                    out_ref[src_ref[t]] += part
                else:
                    j = tgt_ref[t]
                    block = src_ref[t] - first
                    if with_degree:
                        deg_ref[j] += jnp.sum(tile.astype(jnp.float32), axis=1, keepdims=True)

                    @pl.when((block >= 0) & (block < in_count))
                    def _():
                        out_ref[j] += jnp.dot(tile, blocks_ref[block], preferred_element_type=jnp.float32)

            return carry

        lax.fori_loop(0, slots, body, 0)

    whole = lambda i, *_: (0, 0, 0)
    in_specs = [
        pl.BlockSpec(memory_space=pl.ANY),
        pl.BlockSpec((in_count, size, wide), whole),
    ]
    operands = [tile_tgt, tile_src, tile_count, tile_vals, blocks]
    if init is not None:
        in_specs.append(pl.BlockSpec((out_count, size, wide), whole))
        operands.append(init)
    out_specs = [pl.BlockSpec((out_count, size, wide), whole)]
    out_shape = [jax.ShapeDtypeStruct((out_count, size, wide), jnp.float32)]
    if with_degree:
        out_specs.append(pl.BlockSpec((out_count, size, 1), whole))
        out_shape.append(jax.ShapeDtypeStruct((out_count, size, 1), jnp.float32))
    result = pl.pallas_call(
        kernel,
        grid_spec=pltpu.PrefetchScalarGridSpec(
            num_scalar_prefetch=3,
            grid=(1,),
            in_specs=in_specs,
            out_specs=out_specs,
            scratch_shapes=[
                pltpu.VMEM((slots, size, size), tile_vals.dtype),
                pltpu.SemaphoreType.DMA((slots,)),
            ],
        ),
        out_shape=out_shape,
    )(*operands)
    return result if with_degree else result[0]


def per_device(
    features,
    send_dom,
    send_grp,
    tile_vals,
    tile_tgt,
    tile_src,
    tile_count,
    w_self,
    w_neigh,
    cotangent,
):
    tile_size = tile_vals.shape[1]
    width = features.shape[1]
    node_count = features.shape[0]
    block_count = node_count // tile_size
    dom_index = send_dom[0]
    grp_index = send_grp[0]
    n_dom, bnd = dom_index.shape
    n_grp = grp_index.shape[0]
    send_index = jnp.concatenate([dom_index.reshape(-1), grp_index.reshape(-1)])
    pick = one_hot_rows(send_index, node_count)
    sent = jnp.dot(pick, features, preferred_element_type=jnp.float32).astype(jnp.bfloat16)
    sent = sent.reshape(n_dom + n_grp, bnd, width)
    acc_own, degree = tile_pass(
        tile_tgt, tile_src, tile_count, tile_vals, features.reshape(-1, tile_size, width),
        block_count, False,
    )
    recv_dom, recv_grp = exchange(sent[:n_dom], sent[n_dom:])
    received = jnp.concatenate([recv_dom.reshape(-1, width), recv_grp.reshape(-1, width)], axis=0)
    source_count = block_count + received.shape[0] // tile_size
    acc = tile_pass(
        tile_tgt, tile_src, tile_count, tile_vals, received.reshape(-1, tile_size, width),
        block_count, False, first=block_count, init=acc_own,
    )
    agg = (acc / degree).reshape(node_count, width).astype(jnp.bfloat16)
    preact = jnp.dot(features, w_self, preferred_element_type=jnp.float32) + jnp.dot(
        agg, w_neigh, preferred_element_type=jnp.float32
    )
    sigm = jax.nn.sigmoid(preact)
    output = (preact * sigm).astype(jnp.bfloat16)
    grad_pre = (cotangent.astype(jnp.float32) * sigm * (1.0 + preact * (1.0 - sigm))).astype(
        jnp.bfloat16
    )
    part_self = jnp.einsum("nf,nh->fh", features, grad_pre, preferred_element_type=jnp.float32)
    part_neigh = jnp.einsum("nf,nh->fh", agg, grad_pre, preferred_element_type=jnp.float32)
    grad_own = jnp.einsum("nh,fh->nf", grad_pre, w_self, preferred_element_type=jnp.float32)
    grad_agg = jnp.einsum("nh,fh->nf", grad_pre, w_neigh, preferred_element_type=jnp.float32)
    grad_agg = (grad_agg / degree.reshape(-1)[:, None]).astype(jnp.bfloat16)
    grad_source = tile_pass(
        tile_tgt, tile_src, tile_count, tile_vals, grad_agg.reshape(block_count, tile_size, width),
        source_count, True,
    ).reshape(-1, width)
    remote = grad_source[node_count:].astype(jnp.bfloat16).reshape(n_dom + n_grp, bnd, width)
    ret_dom, ret_grp = exchange(remote[:n_dom], remote[n_dom:])
    grad_self, grad_neigh = weight_sum(part_self, part_neigh)
    returned = jnp.concatenate([ret_dom.reshape(-1, width), ret_grp.reshape(-1, width)])
    grad_total = grad_own + grad_source[:node_count]
    grad_total = grad_total + lax.dot_general(
        pick, returned, (((0,), (0,)), ((), ())), preferred_element_type=jnp.float32
    )
    return (output, grad_total.astype(jnp.bfloat16), grad_self, grad_neigh)


def solution(mesh):
    return jax.shard_map(
        per_device,
        mesh=mesh,
        in_specs=(
            P(("dom", "grp"), None),
            P(("dom", "grp"), None, None),
            P(("dom", "grp"), None, None),
            P(("dom", "grp"), None, None),
            P(("dom", "grp")),
            P(("dom", "grp")),
            P(("dom", "grp")),
            P(),
            P(),
            P(("dom", "grp"), None),
        ),
        out_specs=(P(("dom", "grp"), None), P(("dom", "grp"), None), P(), P()),
        check_vma=False,
    )
```

```python
import jax
import jax.numpy as jnp
from jax import lax
from jax.sharding import PartitionSpec as P
from jax.experimental import pallas as pl
from jax.experimental.pallas import tpu as pltpu


def weight_sum(part_self, part_neigh):
    axes = ("dom", "grp")
    peers = lax.psum(1, axes)
    rows = part_self.shape[0]
    stacked = jnp.concatenate([part_self, part_neigh], axis=0)
    flat = stacked.reshape(-1)
    pad = (-flat.shape[0]) % peers
    chunks = jnp.pad(flat, (0, pad)).reshape(peers, -1)
    mine = jnp.sum(lax.all_to_all(chunks, axes, 0, 0, tiled=True), axis=0, keepdims=True)
    spread = jnp.broadcast_to(mine, chunks.shape)
    total = lax.all_to_all(spread, axes, 0, 0, tiled=True).reshape(-1)
    total = total[: flat.shape[0]].reshape(stacked.shape)
    return total[:rows], total[rows:]


def exchange(dom_part, grp_part):
    axes = ("dom", "grp")
    n_dom, n_grp = dom_part.shape[0], grp_part.shape[0]
    a = lax.axis_index("dom")
    b = lax.axis_index("grp")
    cell = dom_part.shape[1:]
    buf = jnp.zeros((n_dom, n_grp) + cell, dom_part.dtype)
    buf = lax.dynamic_update_slice_in_dim(buf, dom_part[:, None], b, axis=1)
    buf = lax.dynamic_update_slice_in_dim(buf, grp_part[None], a, axis=0)
    got = lax.all_to_all(buf.reshape((n_dom * n_grp,) + cell), axes, 0, 0, tiled=True)
    got = got.reshape((n_dom, n_grp) + cell)
    from_dom = lax.dynamic_index_in_dim(got, b, axis=1, keepdims=False)
    own_dom = lax.dynamic_index_in_dim(dom_part, a, axis=0, keepdims=True)
    from_dom = lax.dynamic_update_slice_in_dim(from_dom, own_dom, a, axis=0)
    from_grp = lax.dynamic_index_in_dim(got, a, axis=0, keepdims=False)
    return from_dom, from_grp


def one_hot_rows(index, count):
    return (index.reshape(-1)[:, None] == jnp.arange(count, dtype=jnp.int32)[None, :]).astype(jnp.bfloat16)


def tile_pass(tile_tgt, tile_src, tile_count, tile_vals, blocks, out_count, transpose, first=0, init=None):
    slots, size, _ = tile_vals.shape
    in_count, _, wide = blocks.shape
    diag = in_count if transpose else out_count

    def kernel(tgt_ref, src_ref, cnt_ref, tiles_hbm, blocks_ref, *rest):
        rest = list(rest)
        init_ref = rest.pop(0) if init is not None else None
        out_ref, tiles_buf, sems = rest
        count = cnt_ref[0]
        copies = [
            pltpu.make_async_copy(tiles_hbm.at[t], tiles_buf.at[t], sems.at[t]) for t in range(slots)
        ]
        for c in copies:
            c.start()

        def product(t, read):
            tile = tiles_buf[t]
            if transpose:
                return lax.dot_general(
                    tile, blocks_ref[read], (((0,), (0,)), ((), ())), preferred_element_type=jnp.float32
                )
            return jnp.dot(tile, blocks_ref[read], preferred_element_type=jnp.float32)

        if init is not None:
            out_ref[...] = init_ref[...]
        elif transpose:
            out_ref[diag:] = jnp.zeros((out_count - diag, size, wide), jnp.float32)
        for t in range(diag):
            copies[t].wait()
            if first == 0:
                keep = (t < count).astype(jnp.float32)
                if init is None:
                    out_ref[t] = product(t, t) * keep
                else:
                    out_ref[t] += product(t, t) * keep
        for t in range(diag, slots):
            copies[t].wait()
            if transpose:
                read, write = tgt_ref[t], src_ref[t]
                keep = t < count
            else:
                block = src_ref[t] - first
                keep = (t < count) & (block >= 0) & (block < in_count)
                read, write = jnp.clip(block, 0, in_count - 1), tgt_ref[t]
            out_ref[write] += product(t, read) * keep.astype(jnp.float32)

    whole = lambda i, *_: (0, 0, 0)
    in_specs = [
        pl.BlockSpec(memory_space=pl.ANY),
        pl.BlockSpec((in_count, size, wide), whole),
    ]
    operands = [tile_tgt, tile_src, tile_count, tile_vals, blocks]
    if init is not None:
        in_specs.append(pl.BlockSpec((out_count, size, wide), whole))
        operands.append(init)
    return pl.pallas_call(
        kernel,
        grid_spec=pltpu.PrefetchScalarGridSpec(
            num_scalar_prefetch=3,
            grid=(1,),
            in_specs=in_specs,
            out_specs=pl.BlockSpec((out_count, size, wide), whole),
            scratch_shapes=[
                pltpu.VMEM((slots, size, size), tile_vals.dtype),
                pltpu.SemaphoreType.DMA((slots,)),
            ],
        ),
        out_shape=jax.ShapeDtypeStruct((out_count, size, wide), jnp.float32),
    )(*operands)


def per_device(
    features,
    send_dom,
    send_grp,
    tile_vals,
    tile_tgt,
    tile_src,
    tile_count,
    w_self,
    w_neigh,
    cotangent,
):
    tile_size = tile_vals.shape[1]
    width = features.shape[1]
    node_count = features.shape[0]
    block_count = node_count // tile_size
    dom_index = send_dom[0]
    grp_index = send_grp[0]
    n_dom, bnd = dom_index.shape
    n_grp = grp_index.shape[0]
    send_index = jnp.concatenate([dom_index.reshape(-1), grp_index.reshape(-1)])
    pick = one_hot_rows(send_index, node_count)
    sent = jnp.dot(pick, features, preferred_element_type=jnp.float32).astype(jnp.bfloat16)
    sent = sent.reshape(n_dom + n_grp, bnd, width)
    slot_count = tile_vals.shape[0]
    usable = jnp.arange(slot_count, dtype=jnp.int32) < tile_count[0]
    to_target = (
        (tile_tgt[None, :] == jnp.arange(block_count, dtype=jnp.int32)[:, None]) & usable[None, :]
    ).astype(jnp.float32)
    unit_column = jnp.ones((tile_size,), jnp.bfloat16)
    row_sums = jnp.einsum("tij,j->ti", tile_vals, unit_column, preferred_element_type=jnp.float32)
    degree = jnp.dot(to_target, row_sums, precision=lax.Precision.HIGHEST)[:, :, None]
    acc_own = tile_pass(
        tile_tgt, tile_src, tile_count, tile_vals, features.reshape(-1, tile_size, width),
        block_count, False,
    )
    recv_dom, recv_grp = exchange(sent[:n_dom], sent[n_dom:])
    received = jnp.concatenate([recv_dom.reshape(-1, width), recv_grp.reshape(-1, width)], axis=0)
    source_count = block_count + received.shape[0] // tile_size
    acc = tile_pass(
        tile_tgt, tile_src, tile_count, tile_vals, received.reshape(-1, tile_size, width),
        block_count, False, first=block_count, init=acc_own,
    )
    agg = (acc / degree).reshape(node_count, width).astype(jnp.bfloat16)
    preact = jnp.dot(features, w_self, preferred_element_type=jnp.float32) + jnp.dot(
        agg, w_neigh, preferred_element_type=jnp.float32
    )
    sigm = jax.nn.sigmoid(preact)
    output = (preact * sigm).astype(jnp.bfloat16)
    grad_pre = (cotangent.astype(jnp.float32) * sigm * (1.0 + preact * (1.0 - sigm))).astype(
        jnp.bfloat16
    )
    part_self = jnp.einsum("nf,nh->fh", features, grad_pre, preferred_element_type=jnp.float32)
    part_neigh = jnp.einsum("nf,nh->fh", agg, grad_pre, preferred_element_type=jnp.float32)
    grad_own = jnp.einsum("nh,fh->nf", grad_pre, w_self, preferred_element_type=jnp.float32)
    grad_agg = jnp.einsum("nh,fh->nf", grad_pre, w_neigh, preferred_element_type=jnp.float32)
    grad_agg = (grad_agg / degree.reshape(-1)[:, None]).astype(jnp.bfloat16)
    grad_source = tile_pass(
        tile_tgt, tile_src, tile_count, tile_vals, grad_agg.reshape(block_count, tile_size, width),
        source_count, True,
    ).reshape(-1, width)
    remote = grad_source[node_count:].astype(jnp.bfloat16).reshape(n_dom + n_grp, bnd, width)
    ret_dom, ret_grp = exchange(remote[:n_dom], remote[n_dom:])
    grad_self, grad_neigh = weight_sum(part_self, part_neigh)
    returned = jnp.concatenate([ret_dom.reshape(-1, width), ret_grp.reshape(-1, width)])
    grad_total = grad_own + grad_source[:node_count]
    grad_total = grad_total + lax.dot_general(
        pick, returned, (((0,), (0,)), ((), ())), preferred_element_type=jnp.float32
    )
    return (output, grad_total.astype(jnp.bfloat16), grad_self, grad_neigh)


def solution(mesh):
    return jax.shard_map(
        per_device,
        mesh=mesh,
        in_specs=(
            P(("dom", "grp"), None),
            P(("dom", "grp"), None, None),
            P(("dom", "grp"), None, None),
            P(("dom", "grp"), None, None),
            P(("dom", "grp")),
            P(("dom", "grp")),
            P(("dom", "grp")),
            P(),
            P(),
            P(("dom", "grp"), None),
        ),
        out_specs=(P(("dom", "grp"), None), P(("dom", "grp"), None), P(), P()),
        check_vma=False,
    )
```

```python
import jax
import jax.numpy as jnp
from jax import lax
from jax.sharding import PartitionSpec as P


def weight_sum(part_self, part_neigh):
    axes = ("dom", "grp")
    peers = lax.psum(1, axes)
    rows = part_self.shape[0]
    stacked = jnp.concatenate([part_self, part_neigh], axis=0)
    flat = stacked.reshape(-1)
    pad = (-flat.shape[0]) % peers
    chunks = jnp.pad(flat, (0, pad)).reshape(peers, -1)
    mine = jnp.sum(lax.all_to_all(chunks, axes, 0, 0, tiled=True), axis=0, keepdims=True)
    spread = jnp.broadcast_to(mine, chunks.shape)
    total = lax.all_to_all(spread, axes, 0, 0, tiled=True).reshape(-1)
    total = total[: flat.shape[0]].reshape(stacked.shape)
    return total[:rows], total[rows:]


def exchange(dom_part, grp_part):
    axes = ("dom", "grp")
    n_dom, n_grp = dom_part.shape[0], grp_part.shape[0]
    a = lax.axis_index("dom")
    b = lax.axis_index("grp")
    cell = dom_part.shape[1:]
    buf = jnp.zeros((n_dom, n_grp) + cell, dom_part.dtype)
    buf = lax.dynamic_update_slice_in_dim(buf, dom_part[:, None], b, axis=1)
    buf = lax.dynamic_update_slice_in_dim(buf, grp_part[None], a, axis=0)
    got = lax.all_to_all(buf.reshape((n_dom * n_grp,) + cell), axes, 0, 0, tiled=True)
    got = got.reshape((n_dom, n_grp) + cell)
    from_dom = lax.dynamic_index_in_dim(got, b, axis=1, keepdims=False)
    own_dom = lax.dynamic_index_in_dim(dom_part, a, axis=0, keepdims=True)
    from_dom = lax.dynamic_update_slice_in_dim(from_dom, own_dom, a, axis=0)
    from_grp = lax.dynamic_index_in_dim(got, a, axis=0, keepdims=False)
    return from_dom, from_grp


def one_hot_rows(index, count):
    return (index.reshape(-1)[:, None] == jnp.arange(count, dtype=jnp.int32)[None, :]).astype(jnp.bfloat16)


def per_device(
    features,
    send_dom,
    send_grp,
    tile_vals,
    tile_tgt,
    tile_src,
    tile_count,
    w_self,
    w_neigh,
    cotangent,
):
    tile_size = tile_vals.shape[1]
    width = features.shape[1]
    node_count = features.shape[0]
    block_count = node_count // tile_size
    dom_index = send_dom[0]
    grp_index = send_grp[0]
    n_dom, bnd = dom_index.shape
    n_grp = grp_index.shape[0]
    send_index = jnp.concatenate([dom_index.reshape(-1), grp_index.reshape(-1)])
    pick = one_hot_rows(send_index, node_count)
    sent = jnp.dot(pick, features, preferred_element_type=jnp.float32).astype(jnp.bfloat16)
    sent = sent.reshape(n_dom + n_grp, bnd, width)
    recv_dom, recv_grp = exchange(sent[:n_dom], sent[n_dom:])
    source = jnp.concatenate(
        [features, recv_dom.reshape(-1, width), recv_grp.reshape(-1, width)], axis=0
    )
    source = source.reshape(-1, tile_size, width)
    source_count = source.shape[0]
    slot_count = tile_vals.shape[0]
    usable = jnp.arange(slot_count, dtype=jnp.int32) < tile_count[0]
    target_id = jnp.where(usable, tile_tgt, block_count)
    source_id = jnp.where(usable, tile_src, source_count)
    products = jnp.einsum(
        "tij,tjf->tif", tile_vals, source[tile_src], preferred_element_type=jnp.float32
    )
    summed = jax.ops.segment_sum(products, target_id, num_segments=block_count)
    unit_column = jnp.ones((tile_size,), jnp.bfloat16)
    row_sums = jnp.einsum("tij,j->ti", tile_vals, unit_column, preferred_element_type=jnp.float32)
    degree = jax.ops.segment_sum(row_sums, target_id, num_segments=block_count)
    agg = (summed / degree[:, :, None]).reshape(node_count, width).astype(jnp.bfloat16)
    preact = jnp.dot(features, w_self, preferred_element_type=jnp.float32) + jnp.dot(
        agg, w_neigh, preferred_element_type=jnp.float32
    )
    sigm = jax.nn.sigmoid(preact)
    output = (preact * sigm).astype(jnp.bfloat16)
    grad_pre = (cotangent.astype(jnp.float32) * sigm * (1.0 + preact * (1.0 - sigm))).astype(
        jnp.bfloat16
    )
    part_self = jnp.einsum("nf,nh->fh", features, grad_pre, preferred_element_type=jnp.float32)
    part_neigh = jnp.einsum("nf,nh->fh", agg, grad_pre, preferred_element_type=jnp.float32)
    grad_own = jnp.einsum("nh,fh->nf", grad_pre, w_self, preferred_element_type=jnp.float32)
    grad_agg = jnp.einsum("nh,fh->nf", grad_pre, w_neigh, preferred_element_type=jnp.float32)
    grad_agg = (grad_agg / degree.reshape(-1)[:, None]).astype(jnp.bfloat16)
    picked = grad_agg.reshape(block_count, tile_size, width)[tile_tgt]
    backward = jnp.einsum("tij,tif->tjf", tile_vals, picked, preferred_element_type=jnp.float32)
    grad_source = jax.ops.segment_sum(backward, source_id, num_segments=source_count).reshape(-1, width)
    remote = grad_source[node_count:].astype(jnp.bfloat16).reshape(n_dom + n_grp, bnd, width)
    ret_dom, ret_grp = exchange(remote[:n_dom], remote[n_dom:])
    grad_self, grad_neigh = weight_sum(part_self, part_neigh)
    returned = jnp.concatenate([ret_dom.reshape(-1, width), ret_grp.reshape(-1, width)])
    grad_total = grad_own + grad_source[:node_count]
    grad_total = grad_total + lax.dot_general(
        pick, returned, (((0,), (0,)), ((), ())), preferred_element_type=jnp.float32
    )
    return (output, grad_total.astype(jnp.bfloat16), grad_self, grad_neigh)


def solution(mesh):
    return jax.shard_map(
        per_device,
        mesh=mesh,
        in_specs=(
            P(("dom", "grp"), None),
            P(("dom", "grp"), None, None),
            P(("dom", "grp"), None, None),
            P(("dom", "grp"), None, None),
            P(("dom", "grp")),
            P(("dom", "grp")),
            P(("dom", "grp")),
            P(),
            P(),
            P(("dom", "grp"), None),
        ),
        out_specs=(P(("dom", "grp"), None), P(("dom", "grp"), None), P(), P()),
        check_vma=False,
    )
```

```python
import jax
import jax.numpy as jnp
from jax import lax
from jax.sharding import PartitionSpec as P


def weight_sum(part_self, part_neigh):
    axes = ("dom", "grp")
    peers = lax.psum(1, axes)
    rows = part_self.shape[0]
    stacked = jnp.concatenate([part_self, part_neigh], axis=0)
    flat = stacked.reshape(-1)
    pad = (-flat.shape[0]) % peers
    chunks = jnp.pad(flat, (0, pad)).reshape(peers, -1)
    mine = jnp.sum(lax.all_to_all(chunks, axes, 0, 0, tiled=True), axis=0, keepdims=True)
    spread = jnp.broadcast_to(mine, chunks.shape)
    total = lax.all_to_all(spread, axes, 0, 0, tiled=True).reshape(-1)
    total = total[: flat.shape[0]].reshape(stacked.shape)
    return total[:rows], total[rows:]


def exchange(dom_part, grp_part):
    axes = ("dom", "grp")
    n_dom, n_grp = dom_part.shape[0], grp_part.shape[0]
    a = lax.axis_index("dom")
    b = lax.axis_index("grp")
    cell = dom_part.shape[1:]
    buf = jnp.zeros((n_dom, n_grp) + cell, dom_part.dtype)
    buf = lax.dynamic_update_slice_in_dim(buf, dom_part[:, None], b, axis=1)
    buf = lax.dynamic_update_slice_in_dim(buf, grp_part[None], a, axis=0)
    got = lax.all_to_all(buf.reshape((n_dom * n_grp,) + cell), axes, 0, 0, tiled=True)
    got = got.reshape((n_dom, n_grp) + cell)
    from_dom = lax.dynamic_index_in_dim(got, b, axis=1, keepdims=False)
    own_dom = lax.dynamic_index_in_dim(dom_part, a, axis=0, keepdims=True)
    from_dom = lax.dynamic_update_slice_in_dim(from_dom, own_dom, a, axis=0)
    from_grp = lax.dynamic_index_in_dim(got, a, axis=0, keepdims=False)
    return from_dom, from_grp


ADJ_LIMIT = 4 << 20


def split_bf16(value):
    hi = value.astype(jnp.bfloat16)
    rest = value - hi.astype(jnp.float32)
    mid = rest.astype(jnp.bfloat16)
    low = (rest - mid.astype(jnp.float32)).astype(jnp.bfloat16)
    return hi, mid, low


def one_hot_rows(index, count):
    return (index.reshape(-1)[:, None] == jnp.arange(count, dtype=jnp.int32)[None, :]).astype(jnp.bfloat16)


def per_device(
    features,
    send_dom,
    send_grp,
    tile_vals,
    tile_tgt,
    tile_src,
    tile_count,
    w_self,
    w_neigh,
    cotangent,
):
    tile_size = tile_vals.shape[1]
    width = features.shape[1]
    node_count = features.shape[0]
    block_count = node_count // tile_size
    dom_index = send_dom[0]
    grp_index = send_grp[0]
    n_dom, bnd = dom_index.shape
    n_grp = grp_index.shape[0]
    send_index = jnp.concatenate([dom_index.reshape(-1), grp_index.reshape(-1)])
    pick = one_hot_rows(send_index, node_count)
    sent = jnp.dot(pick, features, preferred_element_type=jnp.float32).astype(jnp.bfloat16)
    sent = sent.reshape(n_dom + n_grp, bnd, width)
    slot_count = tile_vals.shape[0]
    source_count = block_count + (n_dom + n_grp) * bnd // tile_size
    remote_count = source_count - block_count
    usable = jnp.arange(slot_count, dtype=jnp.int32) < tile_count[0]
    to_target = (
        (tile_tgt[None, :] == jnp.arange(block_count, dtype=jnp.int32)[:, None]) & usable[None, :]
    ).astype(jnp.float32)
    unit_column = jnp.ones((tile_size,), jnp.bfloat16)
    row_sums = jnp.einsum("tij,j->ti", tile_vals, unit_column, preferred_element_type=jnp.float32)
    degree = jnp.dot(to_target, row_sums, precision=lax.Precision.HIGHEST)
    split = block_count * remote_count * tile_size * tile_size * 4 <= ADJ_LIMIT
    if split:
        is_own = tile_src < block_count
        own_src = jnp.where(is_own, tile_src, 0)
        own_target = to_target * is_own.astype(jnp.float32)[None, :]
        remote_of = (
            tile_src[None, :] == block_count + jnp.arange(remote_count, dtype=jnp.int32)[:, None]
        ).astype(jnp.float32)
        pair = (to_target[:, None, :] * remote_of[None, :, :]).reshape(-1, slot_count)
        adj = jnp.dot(
            pair.astype(jnp.bfloat16), tile_vals.reshape(slot_count, -1),
            preferred_element_type=jnp.float32,
        )
        adj = adj.reshape(block_count, remote_count, tile_size, tile_size).transpose(0, 2, 1, 3)
        adj = adj.reshape(node_count, remote_count * tile_size)
        pieces = split_bf16(adj)
        own_blocks = features.reshape(block_count, tile_size, width)
        products = jnp.einsum(
            "tij,tjf->tif", tile_vals, own_blocks[own_src], preferred_element_type=jnp.float32
        )
        summed = jnp.einsum("bt,tif->bif", own_target, products, precision=lax.Precision.HIGHEST)
        recv_dom, recv_grp = exchange(sent[:n_dom], sent[n_dom:])
        received = jnp.concatenate([recv_dom.reshape(-1, width), recv_grp.reshape(-1, width)], axis=0)
        far = sum(jnp.dot(p, received, preferred_element_type=jnp.float32) for p in pieces)
        summed = summed.reshape(node_count, width) + far
    else:
        recv_dom, recv_grp = exchange(sent[:n_dom], sent[n_dom:])
        source = jnp.concatenate(
            [features, recv_dom.reshape(-1, width), recv_grp.reshape(-1, width)], axis=0
        )
        source = source.reshape(-1, tile_size, width)
        products = jnp.einsum(
            "tij,tjf->tif", tile_vals, source[tile_src], preferred_element_type=jnp.float32
        )
        summed = jnp.einsum("bt,tif->bif", to_target, products, precision=lax.Precision.HIGHEST)
        summed = summed.reshape(node_count, width)
    agg = (summed / degree.reshape(-1)[:, None]).astype(jnp.bfloat16)
    preact = jnp.dot(features, w_self, preferred_element_type=jnp.float32) + jnp.dot(
        agg, w_neigh, preferred_element_type=jnp.float32
    )
    sigm = jax.nn.sigmoid(preact)
    output = (preact * sigm).astype(jnp.bfloat16)
    grad_pre = (cotangent.astype(jnp.float32) * sigm * (1.0 + preact * (1.0 - sigm))).astype(
        jnp.bfloat16
    )
    part_self = jnp.einsum("nf,nh->fh", features, grad_pre, preferred_element_type=jnp.float32)
    part_neigh = jnp.einsum("nf,nh->fh", agg, grad_pre, preferred_element_type=jnp.float32)
    grad_own = jnp.einsum("nh,fh->nf", grad_pre, w_self, preferred_element_type=jnp.float32)
    grad_agg = jnp.einsum("nh,fh->nf", grad_pre, w_neigh, preferred_element_type=jnp.float32)
    grad_agg = (grad_agg / degree.reshape(-1)[:, None]).astype(jnp.bfloat16)
    picked = grad_agg.reshape(block_count, tile_size, width)[tile_tgt]
    backward = jnp.einsum("tij,tif->tjf", tile_vals, picked, preferred_element_type=jnp.float32)
    if split:
        near = sum(
            lax.dot_general(p, grad_agg, (((0,), (0,)), ((), ())), preferred_element_type=jnp.float32)
            for p in pieces
        )
        to_own = (
            (own_src[None, :] == jnp.arange(block_count, dtype=jnp.int32)[:, None])
            & (usable & is_own)[None, :]
        ).astype(jnp.float32)
        grad_near = jnp.einsum("st,tjf->sjf", to_own, backward, precision=lax.Precision.HIGHEST)
        grad_near = grad_near.reshape(-1, width)
        remote = near.astype(jnp.bfloat16).reshape(n_dom + n_grp, bnd, width)
    else:
        to_source = (
            (tile_src[None, :] == jnp.arange(source_count, dtype=jnp.int32)[:, None]) & usable[None, :]
        ).astype(jnp.float32)
        grad_source = jnp.einsum(
            "st,tjf->sjf", to_source, backward, precision=lax.Precision.HIGHEST
        ).reshape(-1, width)
        grad_near = grad_source[:node_count]
        remote = grad_source[node_count:].astype(jnp.bfloat16).reshape(n_dom + n_grp, bnd, width)
    ret_dom, ret_grp = exchange(remote[:n_dom], remote[n_dom:])
    grad_self, grad_neigh = weight_sum(part_self, part_neigh)
    returned = jnp.concatenate([ret_dom.reshape(-1, width), ret_grp.reshape(-1, width)])
    grad_total = grad_own + grad_near
    grad_total = grad_total + lax.dot_general(
        pick, returned, (((0,), (0,)), ((), ())), preferred_element_type=jnp.float32
    )
    return (output, grad_total.astype(jnp.bfloat16), grad_self, grad_neigh)


def solution(mesh):
    return jax.shard_map(
        per_device,
        mesh=mesh,
        in_specs=(
            P(("dom", "grp"), None),
            P(("dom", "grp"), None, None),
            P(("dom", "grp"), None, None),
            P(("dom", "grp"), None, None),
            P(("dom", "grp")),
            P(("dom", "grp")),
            P(("dom", "grp")),
            P(),
            P(),
            P(("dom", "grp"), None),
        ),
        out_specs=(P(("dom", "grp"), None), P(("dom", "grp"), None), P(), P()),
        check_vma=False,
    )
```

```python
import jax
import jax.numpy as jnp
from jax import lax
from jax.sharding import PartitionSpec as P


def weight_sum(part_self, part_neigh):
    axes = ("dom", "grp")
    peers = lax.psum(1, axes)
    rows = part_self.shape[0]
    stacked = jnp.concatenate([part_self, part_neigh], axis=0)
    flat = stacked.reshape(-1)
    pad = (-flat.shape[0]) % peers
    chunks = jnp.pad(flat, (0, pad)).reshape(peers, -1)
    mine = jnp.sum(lax.all_to_all(chunks, axes, 0, 0, tiled=True), axis=0, keepdims=True)
    spread = jnp.broadcast_to(mine, chunks.shape)
    total = lax.all_to_all(spread, axes, 0, 0, tiled=True).reshape(-1)
    total = total[: flat.shape[0]].reshape(stacked.shape)
    return total[:rows], total[rows:]


def exchange(dom_part, grp_part):
    axes = ("dom", "grp")
    n_dom, n_grp = dom_part.shape[0], grp_part.shape[0]
    a = lax.axis_index("dom")
    b = lax.axis_index("grp")
    cell = dom_part.shape[1:]
    buf = jnp.zeros((n_dom, n_grp) + cell, dom_part.dtype)
    buf = lax.dynamic_update_slice_in_dim(buf, dom_part[:, None], b, axis=1)
    buf = lax.dynamic_update_slice_in_dim(buf, grp_part[None], a, axis=0)
    got = lax.all_to_all(buf.reshape((n_dom * n_grp,) + cell), axes, 0, 0, tiled=True)
    got = got.reshape((n_dom, n_grp) + cell)
    from_dom = lax.dynamic_index_in_dim(got, b, axis=1, keepdims=False)
    own_dom = lax.dynamic_index_in_dim(dom_part, a, axis=0, keepdims=True)
    from_dom = lax.dynamic_update_slice_in_dim(from_dom, own_dom, a, axis=0)
    from_grp = lax.dynamic_index_in_dim(got, a, axis=0, keepdims=False)
    return from_dom, from_grp


def one_hot_rows(index, count):
    hot = index[..., None] == jnp.arange(count, dtype=jnp.int32)
    return hot.astype(jnp.bfloat16).reshape(-1, count)


PLACE_LIMIT = 4 << 20


def placement(n_dom, n_grp, bnd):
    a = lax.axis_index("dom")
    b = lax.axis_index("grp")
    blk = jnp.arange(n_dom + n_grp, dtype=jnp.int32)
    cell = jnp.where(blk < n_dom, blk * n_grp + b, a * n_grp + (blk - n_dom))
    local = blk == a
    cell = jnp.where(local, -1, cell)
    col = cell[:, None] * bnd + jnp.arange(bnd, dtype=jnp.int32)[None, :]
    place = one_hot_rows(col, n_dom * n_grp * bnd)
    keep = jnp.broadcast_to(local[:, None], (n_dom + n_grp, bnd)).reshape(-1, 1)
    return place, keep


def swap(table, place, keep):
    peers = lax.psum(1, ("dom", "grp"))
    buf = lax.dot_general(place, table, (((0,), (0,)), ((), ())), preferred_element_type=jnp.float32)
    buf = buf.astype(table.dtype).reshape(peers, -1, table.shape[1])
    got = lax.all_to_all(buf, ("dom", "grp"), 0, 0, tiled=True).reshape(-1, table.shape[1])
    back = jnp.dot(place, got, preferred_element_type=jnp.float32).astype(table.dtype)
    return jnp.where(keep, table, back)


def per_device(
    features,
    send_dom,
    send_grp,
    tile_vals,
    tile_tgt,
    tile_src,
    tile_count,
    w_self,
    w_neigh,
    cotangent,
):
    tile_size = tile_vals.shape[1]
    width = features.shape[1]
    node_count = features.shape[0]
    block_count = node_count // tile_size
    dom_index = send_dom[0]
    grp_index = send_grp[0]
    n_dom, bnd = dom_index.shape
    n_grp = grp_index.shape[0]
    pick = one_hot_rows(jnp.concatenate([dom_index, grp_index], axis=0), node_count)
    sent = jnp.dot(pick, features, preferred_element_type=jnp.float32).astype(jnp.bfloat16)
    table_bytes = n_dom * n_grp * bnd * (n_dom + n_grp) * bnd * 2
    if table_bytes <= PLACE_LIMIT:
        place, keep = placement(n_dom, n_grp, bnd)
        got = swap(sent, place, keep)
        recv_dom, recv_grp = got[: n_dom * bnd], got[n_dom * bnd :]
    else:
        sent = sent.reshape(n_dom + n_grp, bnd, width)
        recv_dom, recv_grp = exchange(sent[:n_dom], sent[n_dom:])
    source = jnp.concatenate(
        [features, recv_dom.reshape(-1, width), recv_grp.reshape(-1, width)], axis=0
    )
    source = source.reshape(-1, tile_size, width)
    source_count = source.shape[0]
    slot_count = tile_vals.shape[0]
    usable = jnp.arange(slot_count, dtype=jnp.int32) < tile_count[0]
    to_target = (
        (tile_tgt[None, :] == jnp.arange(block_count, dtype=jnp.int32)[:, None]) & usable[None, :]
    ).astype(jnp.float32)
    to_source = (
        (tile_src[None, :] == jnp.arange(source_count, dtype=jnp.int32)[:, None]) & usable[None, :]
    ).astype(jnp.float32)
    products = jnp.einsum(
        "tij,tjf->tif", tile_vals, source[tile_src], preferred_element_type=jnp.float32
    )
    summed = jnp.einsum("bt,tif->bif", to_target, products, precision=lax.Precision.HIGHEST)
    unit_column = jnp.ones((tile_size,), jnp.bfloat16)
    row_sums = jnp.einsum("tij,j->ti", tile_vals, unit_column, preferred_element_type=jnp.float32)
    degree = jnp.dot(to_target, row_sums, precision=lax.Precision.HIGHEST)
    agg = (summed / degree[:, :, None]).reshape(node_count, width).astype(jnp.bfloat16)
    preact = jnp.dot(features, w_self, preferred_element_type=jnp.float32) + jnp.dot(
        agg, w_neigh, preferred_element_type=jnp.float32
    )
    sigm = jax.nn.sigmoid(preact)
    output = (preact * sigm).astype(jnp.bfloat16)
    grad_pre = (cotangent.astype(jnp.float32) * sigm * (1.0 + preact * (1.0 - sigm))).astype(
        jnp.bfloat16
    )
    part_self = jnp.einsum("nf,nh->fh", features, grad_pre, preferred_element_type=jnp.float32)
    part_neigh = jnp.einsum("nf,nh->fh", agg, grad_pre, preferred_element_type=jnp.float32)
    grad_own = jnp.einsum("nh,fh->nf", grad_pre, w_self, preferred_element_type=jnp.float32)
    grad_agg = jnp.einsum("nh,fh->nf", grad_pre, w_neigh, preferred_element_type=jnp.float32)
    grad_agg = (grad_agg / degree.reshape(-1)[:, None]).astype(jnp.bfloat16)
    picked = grad_agg.reshape(block_count, tile_size, width)[tile_tgt]
    backward = jnp.einsum("tij,tif->tjf", tile_vals, picked, preferred_element_type=jnp.float32)
    grad_source = jnp.einsum(
        "st,tjf->sjf", to_source, backward, precision=lax.Precision.HIGHEST
    ).reshape(-1, width)
    remote = grad_source[node_count:].astype(jnp.bfloat16)
    if table_bytes <= PLACE_LIMIT:
        returned = swap(remote, place, keep)
    else:
        remote = remote.reshape(n_dom + n_grp, bnd, width)
        ret_dom, ret_grp = exchange(remote[:n_dom], remote[n_dom:])
        returned = jnp.concatenate([ret_dom.reshape(-1, width), ret_grp.reshape(-1, width)])
    grad_self, grad_neigh = weight_sum(part_self, part_neigh)
    grad_total = grad_own + grad_source[:node_count]
    grad_total = grad_total + lax.dot_general(
        pick, returned, (((0,), (0,)), ((), ())), preferred_element_type=jnp.float32
    )
    return (output, grad_total.astype(jnp.bfloat16), grad_self, grad_neigh)


def solution(mesh):
    return jax.shard_map(
        per_device,
        mesh=mesh,
        in_specs=(
            P(("dom", "grp"), None),
            P(("dom", "grp"), None, None),
            P(("dom", "grp"), None, None),
            P(("dom", "grp"), None, None),
            P(("dom", "grp")),
            P(("dom", "grp")),
            P(("dom", "grp")),
            P(),
            P(),
            P(("dom", "grp"), None),
        ),
        out_specs=(P(("dom", "grp"), None), P(("dom", "grp"), None), P(), P()),
        check_vma=False,
    )
```

```python
import jax
import jax.numpy as jnp
from jax import lax
from jax.sharding import PartitionSpec as P


def weight_sum(part_self, part_neigh, stacked=None):
    axes = ("dom", "grp")
    peers = lax.psum(1, axes)
    rows = part_self.shape[0]
    if stacked is None:
        stacked = jnp.concatenate([part_self, part_neigh], axis=0)
    if stacked.shape[0] % (8 * peers) == 0:
        chunks = stacked.reshape(peers, -1, stacked.shape[1])
        mine = jnp.sum(lax.all_to_all(chunks, axes, 0, 0, tiled=True), axis=0, keepdims=True)
        total = lax.all_to_all(jnp.broadcast_to(mine, chunks.shape), axes, 0, 0, tiled=True)
        total = total.reshape(stacked.shape)
        return total[:rows], total[rows:]
    flat = stacked.reshape(-1)
    pad = (-flat.shape[0]) % peers
    chunks = jnp.pad(flat, (0, pad)).reshape(peers, -1)
    mine = jnp.sum(lax.all_to_all(chunks, axes, 0, 0, tiled=True), axis=0, keepdims=True)
    spread = jnp.broadcast_to(mine, chunks.shape)
    total = lax.all_to_all(spread, axes, 0, 0, tiled=True).reshape(-1)
    total = total[: flat.shape[0]].reshape(stacked.shape)
    return total[:rows], total[rows:]


def exchange(dom_part, grp_part):
    axes = ("dom", "grp")
    n_dom, n_grp = dom_part.shape[0], grp_part.shape[0]
    a = lax.axis_index("dom")
    b = lax.axis_index("grp")
    cell = dom_part.shape[1:]
    buf = jnp.zeros((n_dom, n_grp) + cell, dom_part.dtype)
    buf = lax.dynamic_update_slice_in_dim(buf, dom_part[:, None], b, axis=1)
    buf = lax.dynamic_update_slice_in_dim(buf, grp_part[None], a, axis=0)
    got = lax.all_to_all(buf.reshape((n_dom * n_grp,) + cell), axes, 0, 0, tiled=True)
    got = got.reshape((n_dom, n_grp) + cell)
    from_dom = lax.dynamic_index_in_dim(got, b, axis=1, keepdims=False)
    own_dom = lax.dynamic_index_in_dim(dom_part, a, axis=0, keepdims=True)
    from_dom = lax.dynamic_update_slice_in_dim(from_dom, own_dom, a, axis=0)
    from_grp = lax.dynamic_index_in_dim(got, a, axis=0, keepdims=False)
    return from_dom, from_grp


def one_hot_rows(index, count):
    hot = index[..., None] == jnp.arange(count, dtype=jnp.int32)
    return hot.astype(jnp.bfloat16).reshape(-1, count)


PLACE_LIMIT = 4 << 20


def placement(n_dom, n_grp, bnd):
    a = lax.axis_index("dom")
    b = lax.axis_index("grp")
    blk = jnp.arange(n_dom + n_grp, dtype=jnp.int32)
    cell = jnp.where(blk < n_dom, blk * n_grp + b, a * n_grp + (blk - n_dom))
    local = blk == a
    cell = jnp.where(local, -1, cell)
    col = cell[:, None] * bnd + jnp.arange(bnd, dtype=jnp.int32)[None, :]
    place = one_hot_rows(col, n_dom * n_grp * bnd)
    keep = jnp.broadcast_to(local[:, None], (n_dom + n_grp, bnd)).reshape(-1, 1)
    return place, keep


def swap(table, place, keep, buf=None):
    peers = lax.psum(1, ("dom", "grp"))
    if buf is None:
        buf = lax.dot_general(place, table, (((0,), (0,)), ((), ())), preferred_element_type=jnp.float32)
        buf = buf.astype(table.dtype)
    buf = buf.reshape(peers, -1, table.shape[1])
    got = lax.all_to_all(buf, ("dom", "grp"), 0, 0, tiled=True).reshape(-1, table.shape[1])
    back = jnp.dot(place, got, preferred_element_type=jnp.float32).astype(table.dtype)
    return jnp.where(keep, table, back)


def send_rows(dom_index, grp_index):
    a = lax.axis_index("dom")
    b = lax.axis_index("grp")
    n_dom, n_grp = dom_index.shape[0], grp_index.shape[0]
    p = jnp.arange(n_dom, dtype=jnp.int32)[:, None, None]
    q = jnp.arange(n_grp, dtype=jnp.int32)[None, :, None]
    return jnp.where(p == a, grp_index[None], jnp.where(q == b, dom_index[:, None], -1))


def per_device(
    features,
    send_dom,
    send_grp,
    tile_vals,
    tile_tgt,
    tile_src,
    tile_count,
    w_self,
    w_neigh,
    cotangent,
):
    tile_size = tile_vals.shape[1]
    width = features.shape[1]
    node_count = features.shape[0]
    block_count = node_count // tile_size
    dom_index = send_dom[0]
    grp_index = send_grp[0]
    n_dom, bnd = dom_index.shape
    n_grp = grp_index.shape[0]
    pick = one_hot_rows(jnp.concatenate([dom_index, grp_index], axis=0), node_count)
    table_bytes = n_dom * n_grp * bnd * (n_dom + n_grp) * bnd * 2
    if table_bytes <= PLACE_LIMIT:
        place, keep = placement(n_dom, n_grp, bnd)
        direct = one_hot_rows(send_rows(dom_index, grp_index), node_count)
        buf = jnp.dot(direct, features, preferred_element_type=jnp.float32).astype(jnp.bfloat16)
        own_rows = one_hot_rows(lax.dynamic_index_in_dim(dom_index, lax.axis_index("dom"), 0), node_count)
        own_sent = jnp.dot(own_rows, features, preferred_element_type=jnp.float32).astype(jnp.bfloat16)
        table = jnp.zeros(((n_dom + n_grp) * bnd, width), jnp.bfloat16)
        table = lax.dynamic_update_slice_in_dim(table, own_sent, lax.axis_index("dom") * bnd, 0)
        got = swap(table, place, keep, buf)
        recv_dom, recv_grp = got[: n_dom * bnd], got[n_dom * bnd :]
    else:
        sent = jnp.dot(pick, features, preferred_element_type=jnp.float32).astype(jnp.bfloat16)
        sent = sent.reshape(n_dom + n_grp, bnd, width)
        recv_dom, recv_grp = exchange(sent[:n_dom], sent[n_dom:])
    source = jnp.concatenate(
        [features, recv_dom.reshape(-1, width), recv_grp.reshape(-1, width)], axis=0
    )
    source = source.reshape(-1, tile_size, width)
    source_count = source.shape[0]
    slot_count = tile_vals.shape[0]
    usable = jnp.arange(slot_count, dtype=jnp.int32) < tile_count[0]
    to_target = (
        (tile_tgt[None, :] == jnp.arange(block_count, dtype=jnp.int32)[:, None]) & usable[None, :]
    ).astype(jnp.float32)
    to_source = (
        (tile_src[None, :] == jnp.arange(source_count, dtype=jnp.int32)[:, None]) & usable[None, :]
    ).astype(jnp.float32)
    products = jnp.einsum(
        "tij,tjf->tif", tile_vals, source[tile_src], preferred_element_type=jnp.float32
    )
    summed = jnp.einsum("bt,tif->bif", to_target, products, precision=lax.Precision.HIGHEST)
    unit_column = jnp.ones((tile_size,), jnp.bfloat16)
    row_sums = jnp.einsum("tij,j->ti", tile_vals, unit_column, preferred_element_type=jnp.float32)
    degree = jnp.dot(to_target, row_sums, precision=lax.Precision.HIGHEST)
    agg = (summed / degree[:, :, None]).reshape(node_count, width).astype(jnp.bfloat16)
    preact = jnp.dot(features, w_self, preferred_element_type=jnp.float32) + jnp.dot(
        agg, w_neigh, preferred_element_type=jnp.float32
    )
    sigm = jax.nn.sigmoid(preact)
    output = (preact * sigm).astype(jnp.bfloat16)
    grad_pre = (cotangent.astype(jnp.float32) * sigm * (1.0 + preact * (1.0 - sigm))).astype(
        jnp.bfloat16
    )
    stacked = jnp.einsum(
        "nf,nh->fh", jnp.concatenate([features, agg], axis=1), grad_pre,
        preferred_element_type=jnp.float32,
    )
    part_self, part_neigh = stacked[:width], stacked[width:]
    grad_own = jnp.einsum("nh,fh->nf", grad_pre, w_self, preferred_element_type=jnp.float32)
    grad_agg = jnp.einsum("nh,fh->nf", grad_pre, w_neigh, preferred_element_type=jnp.float32)
    grad_agg = (grad_agg / degree.reshape(-1)[:, None]).astype(jnp.bfloat16)
    picked = grad_agg.reshape(block_count, tile_size, width)[tile_tgt]
    backward = jnp.einsum("tij,tif->tjf", tile_vals, picked, preferred_element_type=jnp.float32)
    grad_source = jnp.einsum(
        "st,tjf->sjf", to_source, backward, precision=lax.Precision.HIGHEST
    ).reshape(-1, width)
    remote = grad_source[node_count:].astype(jnp.bfloat16)
    if table_bytes <= PLACE_LIMIT:
        returned = swap(remote, place, keep)
    else:
        remote = remote.reshape(n_dom + n_grp, bnd, width)
        ret_dom, ret_grp = exchange(remote[:n_dom], remote[n_dom:])
        returned = jnp.concatenate([ret_dom.reshape(-1, width), ret_grp.reshape(-1, width)])
    grad_self, grad_neigh = weight_sum(part_self, part_neigh, stacked)
    grad_total = grad_own + grad_source[:node_count]
    grad_total = grad_total + lax.dot_general(
        pick, returned, (((0,), (0,)), ((), ())), preferred_element_type=jnp.float32
    )
    return (output, grad_total.astype(jnp.bfloat16), grad_self, grad_neigh)


def solution(mesh):
    return jax.shard_map(
        per_device,
        mesh=mesh,
        in_specs=(
            P(("dom", "grp"), None),
            P(("dom", "grp"), None, None),
            P(("dom", "grp"), None, None),
            P(("dom", "grp"), None, None),
            P(("dom", "grp")),
            P(("dom", "grp")),
            P(("dom", "grp")),
            P(),
            P(),
            P(("dom", "grp"), None),
        ),
        out_specs=(P(("dom", "grp"), None), P(("dom", "grp"), None), P(), P()),
        check_vma=False,
    )
```

```python
import jax
import jax.numpy as jnp
from jax import lax
from jax.sharding import PartitionSpec as P


def weight_sum(part_self, part_neigh, stacked=None):
    axes = ("dom", "grp")
    peers = lax.psum(1, axes)
    rows = part_self.shape[0]
    if stacked is None:
        stacked = jnp.concatenate([part_self, part_neigh], axis=0)
    if stacked.shape[0] % (8 * peers) == 0:
        chunks = stacked.reshape(peers, -1, stacked.shape[1])
        mine = jnp.sum(lax.all_to_all(chunks, axes, 0, 0, tiled=True), axis=0, keepdims=True)
        total = lax.all_to_all(jnp.broadcast_to(mine, chunks.shape), axes, 0, 0, tiled=True)
        total = total.reshape(stacked.shape)
        return total[:rows], total[rows:]
    flat = stacked.reshape(-1)
    pad = (-flat.shape[0]) % peers
    chunks = jnp.pad(flat, (0, pad)).reshape(peers, -1)
    mine = jnp.sum(lax.all_to_all(chunks, axes, 0, 0, tiled=True), axis=0, keepdims=True)
    spread = jnp.broadcast_to(mine, chunks.shape)
    total = lax.all_to_all(spread, axes, 0, 0, tiled=True).reshape(-1)
    total = total[: flat.shape[0]].reshape(stacked.shape)
    return total[:rows], total[rows:]


def exchange(dom_part, grp_part):
    axes = ("dom", "grp")
    n_dom, n_grp = dom_part.shape[0], grp_part.shape[0]
    a = lax.axis_index("dom")
    b = lax.axis_index("grp")
    cell = dom_part.shape[1:]
    buf = jnp.zeros((n_dom, n_grp) + cell, dom_part.dtype)
    buf = lax.dynamic_update_slice_in_dim(buf, dom_part[:, None], b, axis=1)
    buf = lax.dynamic_update_slice_in_dim(buf, grp_part[None], a, axis=0)
    got = lax.all_to_all(buf.reshape((n_dom * n_grp,) + cell), axes, 0, 0, tiled=True)
    got = got.reshape((n_dom, n_grp) + cell)
    from_dom = lax.dynamic_index_in_dim(got, b, axis=1, keepdims=False)
    own_dom = lax.dynamic_index_in_dim(dom_part, a, axis=0, keepdims=True)
    from_dom = lax.dynamic_update_slice_in_dim(from_dom, own_dom, a, axis=0)
    from_grp = lax.dynamic_index_in_dim(got, a, axis=0, keepdims=False)
    return from_dom, from_grp


def one_hot_rows(index, count):
    hot = index[..., None] == jnp.arange(count, dtype=jnp.int32)
    return hot.astype(jnp.bfloat16).reshape(-1, count)


PLACE_LIMIT = 4 << 20


def placement(n_dom, n_grp, bnd):
    a = lax.axis_index("dom")
    b = lax.axis_index("grp")
    blk = jnp.arange(n_dom + n_grp, dtype=jnp.int32)
    cell = jnp.where(blk < n_dom, blk * n_grp + b, a * n_grp + (blk - n_dom))
    local = blk == a
    cell = jnp.where(local, -1, cell)
    col = cell[:, None] * bnd + jnp.arange(bnd, dtype=jnp.int32)[None, :]
    place = one_hot_rows(col, n_dom * n_grp * bnd)
    keep = jnp.broadcast_to(local[:, None], (n_dom + n_grp, bnd)).reshape(-1, 1)
    return place, keep


def swap(table, place, keep):
    peers = lax.psum(1, ("dom", "grp"))
    buf = lax.dot_general(place, table, (((0,), (0,)), ((), ())), preferred_element_type=jnp.float32)
    buf = buf.astype(table.dtype).reshape(peers, -1, table.shape[1])
    got = lax.all_to_all(buf, ("dom", "grp"), 0, 0, tiled=True).reshape(-1, table.shape[1])
    back = jnp.dot(place, got, preferred_element_type=jnp.float32).astype(table.dtype)
    return jnp.where(keep, table, back)


def per_device(
    features,
    send_dom,
    send_grp,
    tile_vals,
    tile_tgt,
    tile_src,
    tile_count,
    w_self,
    w_neigh,
    cotangent,
):
    tile_size = tile_vals.shape[1]
    width = features.shape[1]
    node_count = features.shape[0]
    block_count = node_count // tile_size
    dom_index = send_dom[0]
    grp_index = send_grp[0]
    n_dom, bnd = dom_index.shape
    n_grp = grp_index.shape[0]
    pick = one_hot_rows(jnp.concatenate([dom_index, grp_index], axis=0), node_count)
    sent = jnp.dot(pick, features, preferred_element_type=jnp.float32).astype(jnp.bfloat16)
    table_bytes = n_dom * n_grp * bnd * (n_dom + n_grp) * bnd * 2
    if table_bytes <= PLACE_LIMIT:
        place, keep = placement(n_dom, n_grp, bnd)
        got = swap(sent, place, keep)
        recv_dom, recv_grp = got[: n_dom * bnd], got[n_dom * bnd :]
    else:
        sent = sent.reshape(n_dom + n_grp, bnd, width)
        recv_dom, recv_grp = exchange(sent[:n_dom], sent[n_dom:])
    source = jnp.concatenate(
        [features, recv_dom.reshape(-1, width), recv_grp.reshape(-1, width)], axis=0
    )
    source = source.reshape(-1, tile_size, width)
    source_count = source.shape[0]
    slot_count = tile_vals.shape[0]
    usable = jnp.arange(slot_count, dtype=jnp.int32) < tile_count[0]
    to_target = (
        (tile_tgt[None, :] == jnp.arange(block_count, dtype=jnp.int32)[:, None]) & usable[None, :]
    ).astype(jnp.float32)
    to_source = (
        (tile_src[None, :] == jnp.arange(source_count, dtype=jnp.int32)[:, None]) & usable[None, :]
    ).astype(jnp.float32)
    products = jnp.einsum(
        "tij,tjf->tif", tile_vals, source[tile_src], preferred_element_type=jnp.float32
    )
    summed = jnp.einsum("bt,tif->bif", to_target, products, precision=lax.Precision.HIGHEST)
    unit_column = jnp.ones((tile_size,), jnp.bfloat16)
    row_sums = jnp.einsum("tij,j->ti", tile_vals, unit_column, preferred_element_type=jnp.float32)
    degree = jnp.dot(to_target, row_sums, precision=lax.Precision.HIGHEST)
    agg = (summed / degree[:, :, None]).reshape(node_count, width).astype(jnp.bfloat16)
    preact = jnp.dot(features, w_self, preferred_element_type=jnp.float32) + jnp.dot(
        agg, w_neigh, preferred_element_type=jnp.float32
    )
    sigm = jax.nn.sigmoid(preact)
    output = (preact * sigm).astype(jnp.bfloat16)
    grad_pre = (cotangent.astype(jnp.float32) * sigm * (1.0 + preact * (1.0 - sigm))).astype(
        jnp.bfloat16
    )
    stacked = jnp.einsum(
        "nf,nh->fh", jnp.concatenate([features, agg], axis=1), grad_pre,
        preferred_element_type=jnp.float32,
    )
    part_self, part_neigh = stacked[:width], stacked[width:]
    grad_own = jnp.einsum("nh,fh->nf", grad_pre, w_self, preferred_element_type=jnp.float32)
    grad_agg = jnp.einsum("nh,fh->nf", grad_pre, w_neigh, preferred_element_type=jnp.float32)
    grad_agg = (grad_agg / degree.reshape(-1)[:, None]).astype(jnp.bfloat16)
    picked = grad_agg.reshape(block_count, tile_size, width)[tile_tgt]
    backward = jnp.einsum("tij,tif->tjf", tile_vals, picked, preferred_element_type=jnp.float32)
    grad_source = jnp.einsum(
        "st,tjf->sjf", to_source, backward, precision=lax.Precision.HIGHEST
    ).reshape(-1, width)
    remote = grad_source[node_count:].astype(jnp.bfloat16)
    if table_bytes <= PLACE_LIMIT:
        returned = swap(remote, place, keep)
    else:
        remote = remote.reshape(n_dom + n_grp, bnd, width)
        ret_dom, ret_grp = exchange(remote[:n_dom], remote[n_dom:])
        returned = jnp.concatenate([ret_dom.reshape(-1, width), ret_grp.reshape(-1, width)])
    grad_self, grad_neigh = weight_sum(part_self, part_neigh, stacked)
    grad_total = grad_own + grad_source[:node_count]
    grad_total = grad_total + lax.dot_general(
        pick, returned, (((0,), (0,)), ((), ())), preferred_element_type=jnp.float32
    )
    return (output, grad_total.astype(jnp.bfloat16), grad_self, grad_neigh)


def solution(mesh):
    return jax.shard_map(
        per_device,
        mesh=mesh,
        in_specs=(
            P(("dom", "grp"), None),
            P(("dom", "grp"), None, None),
            P(("dom", "grp"), None, None),
            P(("dom", "grp"), None, None),
            P(("dom", "grp")),
            P(("dom", "grp")),
            P(("dom", "grp")),
            P(),
            P(),
            P(("dom", "grp"), None),
        ),
        out_specs=(P(("dom", "grp"), None), P(("dom", "grp"), None), P(), P()),
        check_vma=False,
    )
```

```python
import jax
import jax.numpy as jnp
from jax import lax
from jax.sharding import PartitionSpec as P


def weight_sum(part_self, part_neigh):
    axes = ("dom", "grp")
    peers = lax.psum(1, axes)
    rows = part_self.shape[0]
    stacked = jnp.concatenate([part_self, part_neigh], axis=0)
    flat = stacked.reshape(-1)
    pad = (-flat.shape[0]) % peers
    chunks = jnp.pad(flat, (0, pad)).reshape(peers, -1)
    mine = jnp.sum(lax.all_to_all(chunks, axes, 0, 0, tiled=True), axis=0, keepdims=True)
    spread = jnp.broadcast_to(mine, chunks.shape)
    total = lax.all_to_all(spread, axes, 0, 0, tiled=True).reshape(-1)
    total = total[: flat.shape[0]].reshape(stacked.shape)
    return total[:rows], total[rows:]


def exchange(dom_part, grp_part):
    axes = ("dom", "grp")
    n_dom, n_grp = dom_part.shape[0], grp_part.shape[0]
    a = lax.axis_index("dom")
    b = lax.axis_index("grp")
    cell = dom_part.shape[1:]
    buf = jnp.zeros((n_dom, n_grp) + cell, dom_part.dtype)
    buf = lax.dynamic_update_slice_in_dim(buf, dom_part[:, None], b, axis=1)
    buf = lax.dynamic_update_slice_in_dim(buf, grp_part[None], a, axis=0)
    got = lax.all_to_all(buf.reshape((n_dom * n_grp,) + cell), axes, 0, 0, tiled=True)
    got = got.reshape((n_dom, n_grp) + cell)
    from_dom = lax.dynamic_index_in_dim(got, b, axis=1, keepdims=False)
    own_dom = lax.dynamic_index_in_dim(dom_part, a, axis=0, keepdims=True)
    from_dom = lax.dynamic_update_slice_in_dim(from_dom, own_dom, a, axis=0)
    from_grp = lax.dynamic_index_in_dim(got, a, axis=0, keepdims=False)
    return from_dom, from_grp


def segment_matmul(hot, values):
    hi = values.astype(jnp.bfloat16)
    lo = (values - hi.astype(jnp.float32)).astype(jnp.bfloat16)
    hot = hot.astype(jnp.bfloat16)
    first = jnp.einsum("bt,t...->b...", hot, hi, preferred_element_type=jnp.float32)
    return first + jnp.einsum("bt,t...->b...", hot, lo, preferred_element_type=jnp.float32)


def one_hot_rows(index, count):
    hot = index[..., None] == jnp.arange(count, dtype=jnp.int32)
    return hot.astype(jnp.bfloat16).reshape(-1, count)


PLACE_LIMIT = 4 << 20


def placement(n_dom, n_grp, bnd):
    a = lax.axis_index("dom")
    b = lax.axis_index("grp")
    blk = jnp.arange(n_dom + n_grp, dtype=jnp.int32)
    cell = jnp.where(blk < n_dom, blk * n_grp + b, a * n_grp + (blk - n_dom))
    local = blk == a
    cell = jnp.where(local, -1, cell)
    col = cell[:, None] * bnd + jnp.arange(bnd, dtype=jnp.int32)[None, :]
    place = one_hot_rows(col, n_dom * n_grp * bnd)
    keep = jnp.broadcast_to(local[:, None], (n_dom + n_grp, bnd)).reshape(-1, 1)
    return place, keep


def swap(table, place, keep):
    peers = lax.psum(1, ("dom", "grp"))
    buf = lax.dot_general(place, table, (((0,), (0,)), ((), ())), preferred_element_type=jnp.float32)
    buf = buf.astype(table.dtype).reshape(peers, -1, table.shape[1])
    got = lax.all_to_all(buf, ("dom", "grp"), 0, 0, tiled=True).reshape(-1, table.shape[1])
    back = jnp.dot(place, got, preferred_element_type=jnp.float32).astype(table.dtype)
    return jnp.where(keep, table, back)


def per_device(
    features,
    send_dom,
    send_grp,
    tile_vals,
    tile_tgt,
    tile_src,
    tile_count,
    w_self,
    w_neigh,
    cotangent,
):
    tile_size = tile_vals.shape[1]
    width = features.shape[1]
    node_count = features.shape[0]
    block_count = node_count // tile_size
    dom_index = send_dom[0]
    grp_index = send_grp[0]
    n_dom, bnd = dom_index.shape
    n_grp = grp_index.shape[0]
    pick = one_hot_rows(jnp.concatenate([dom_index, grp_index], axis=0), node_count)
    sent = jnp.dot(pick, features, preferred_element_type=jnp.float32).astype(jnp.bfloat16)
    table_bytes = n_dom * n_grp * bnd * (n_dom + n_grp) * bnd * 2
    if table_bytes <= PLACE_LIMIT:
        place, keep = placement(n_dom, n_grp, bnd)
        got = swap(sent, place, keep)
        recv_dom, recv_grp = got[: n_dom * bnd], got[n_dom * bnd :]
    else:
        sent = sent.reshape(n_dom + n_grp, bnd, width)
        recv_dom, recv_grp = exchange(sent[:n_dom], sent[n_dom:])
    source = jnp.concatenate(
        [features, recv_dom.reshape(-1, width), recv_grp.reshape(-1, width)], axis=0
    )
    source = source.reshape(-1, tile_size, width)
    source_count = source.shape[0]
    slot_count = tile_vals.shape[0]
    usable = jnp.arange(slot_count, dtype=jnp.int32) < tile_count[0]
    to_target = (
        (tile_tgt[None, :] == jnp.arange(block_count, dtype=jnp.int32)[:, None]) & usable[None, :]
    ).astype(jnp.float32)
    to_source = (
        (tile_src[None, :] == jnp.arange(source_count, dtype=jnp.int32)[:, None]) & usable[None, :]
    ).astype(jnp.float32)
    products = jnp.einsum(
        "tij,tjf->tif", tile_vals, source[tile_src], preferred_element_type=jnp.float32
    )
    summed = segment_matmul(to_target, products)
    unit_column = jnp.ones((tile_size,), jnp.bfloat16)
    row_sums = jnp.einsum("tij,j->ti", tile_vals, unit_column, preferred_element_type=jnp.float32)
    degree = jnp.dot(to_target, row_sums, precision=lax.Precision.HIGHEST)
    agg = (summed / degree[:, :, None]).reshape(node_count, width).astype(jnp.bfloat16)
    preact = jnp.dot(features, w_self, preferred_element_type=jnp.float32) + jnp.dot(
        agg, w_neigh, preferred_element_type=jnp.float32
    )
    sigm = jax.nn.sigmoid(preact)
    output = (preact * sigm).astype(jnp.bfloat16)
    grad_pre = (cotangent.astype(jnp.float32) * sigm * (1.0 + preact * (1.0 - sigm))).astype(
        jnp.bfloat16
    )
    part_self = jnp.einsum("nf,nh->fh", features, grad_pre, preferred_element_type=jnp.float32)
    part_neigh = jnp.einsum("nf,nh->fh", agg, grad_pre, preferred_element_type=jnp.float32)
    grad_own = jnp.einsum("nh,fh->nf", grad_pre, w_self, preferred_element_type=jnp.float32)
    grad_agg = jnp.einsum("nh,fh->nf", grad_pre, w_neigh, preferred_element_type=jnp.float32)
    grad_agg = (grad_agg / degree.reshape(-1)[:, None]).astype(jnp.bfloat16)
    picked = grad_agg.reshape(block_count, tile_size, width)[tile_tgt]
    backward = jnp.einsum("tij,tif->tjf", tile_vals, picked, preferred_element_type=jnp.float32)
    grad_source = segment_matmul(to_source, backward).reshape(-1, width)
    remote = grad_source[node_count:].astype(jnp.bfloat16)
    if table_bytes <= PLACE_LIMIT:
        returned = swap(remote, place, keep)
    else:
        remote = remote.reshape(n_dom + n_grp, bnd, width)
        ret_dom, ret_grp = exchange(remote[:n_dom], remote[n_dom:])
        returned = jnp.concatenate([ret_dom.reshape(-1, width), ret_grp.reshape(-1, width)])
    grad_self, grad_neigh = weight_sum(part_self, part_neigh)
    grad_total = grad_own + grad_source[:node_count]
    grad_total = grad_total + lax.dot_general(
        pick, returned, (((0,), (0,)), ((), ())), preferred_element_type=jnp.float32
    )
    return (output, grad_total.astype(jnp.bfloat16), grad_self, grad_neigh)


def solution(mesh):
    return jax.shard_map(
        per_device,
        mesh=mesh,
        in_specs=(
            P(("dom", "grp"), None),
            P(("dom", "grp"), None, None),
            P(("dom", "grp"), None, None),
            P(("dom", "grp"), None, None),
            P(("dom", "grp")),
            P(("dom", "grp")),
            P(("dom", "grp")),
            P(),
            P(),
            P(("dom", "grp"), None),
        ),
        out_specs=(P(("dom", "grp"), None), P(("dom", "grp"), None), P(), P()),
        check_vma=False,
    )
```

```python
import jax
import jax.numpy as jnp
from jax import lax
from jax.sharding import PartitionSpec as P


def weight_sum(part_self, part_neigh):
    axes = ("dom", "grp")
    peers = lax.psum(1, axes)
    rows = part_self.shape[0]
    stacked = jnp.concatenate([part_self, part_neigh], axis=0)
    flat = stacked.reshape(-1)
    pad = (-flat.shape[0]) % peers
    chunks = jnp.pad(flat, (0, pad)).reshape(peers, -1)
    mine = jnp.sum(lax.all_to_all(chunks, axes, 0, 0, tiled=True), axis=0, keepdims=True)
    spread = jnp.broadcast_to(mine, chunks.shape)
    total = lax.all_to_all(spread, axes, 0, 0, tiled=True).reshape(-1)
    total = total[: flat.shape[0]].reshape(stacked.shape)
    return total[:rows], total[rows:]


def exchange(dom_part, grp_part):
    axes = ("dom", "grp")
    n_dom, n_grp = dom_part.shape[0], grp_part.shape[0]
    a = lax.axis_index("dom")
    b = lax.axis_index("grp")
    cell = dom_part.shape[1:]
    buf = jnp.zeros((n_dom, n_grp) + cell, dom_part.dtype)
    buf = lax.dynamic_update_slice_in_dim(buf, dom_part[:, None], b, axis=1)
    buf = lax.dynamic_update_slice_in_dim(buf, grp_part[None], a, axis=0)
    got = lax.all_to_all(buf.reshape((n_dom * n_grp,) + cell), axes, 0, 0, tiled=True)
    got = got.reshape((n_dom, n_grp) + cell)
    from_dom = lax.dynamic_index_in_dim(got, b, axis=1, keepdims=False)
    own_dom = lax.dynamic_index_in_dim(dom_part, a, axis=0, keepdims=True)
    from_dom = lax.dynamic_update_slice_in_dim(from_dom, own_dom, a, axis=0)
    from_grp = lax.dynamic_index_in_dim(got, a, axis=0, keepdims=False)
    return from_dom, from_grp


def one_hot_rows(index, count):
    hot = index[..., None] == jnp.arange(count, dtype=jnp.int32)
    return hot.astype(jnp.bfloat16).reshape(-1, count)


PLACE_LIMIT = 4 << 20


def placement(n_dom, n_grp, bnd):
    a = lax.axis_index("dom")
    b = lax.axis_index("grp")
    blk = jnp.arange(n_dom + n_grp, dtype=jnp.int32)
    cell = jnp.where(blk < n_dom, blk * n_grp + b, a * n_grp + (blk - n_dom))
    local = blk == a
    cell = jnp.where(local, -1, cell)
    col = cell[:, None] * bnd + jnp.arange(bnd, dtype=jnp.int32)[None, :]
    place = one_hot_rows(col, n_dom * n_grp * bnd)
    keep = jnp.broadcast_to(local[:, None], (n_dom + n_grp, bnd)).reshape(-1, 1)
    return place, keep


def swap(table, place, keep):
    peers = lax.psum(1, ("dom", "grp"))
    buf = lax.dot_general(place, table, (((0,), (0,)), ((), ())), preferred_element_type=jnp.float32)
    buf = buf.astype(table.dtype).reshape(peers, -1, table.shape[1])
    got = lax.all_to_all(buf, ("dom", "grp"), 0, 0, tiled=True).reshape(-1, table.shape[1])
    back = jnp.dot(place, got, preferred_element_type=jnp.float32).astype(table.dtype)
    return jnp.where(keep, table, back)


def per_device(
    features,
    send_dom,
    send_grp,
    tile_vals,
    tile_tgt,
    tile_src,
    tile_count,
    w_self,
    w_neigh,
    cotangent,
):
    tile_size = tile_vals.shape[1]
    width = features.shape[1]
    node_count = features.shape[0]
    block_count = node_count // tile_size
    dom_index = send_dom[0]
    grp_index = send_grp[0]
    n_dom, bnd = dom_index.shape
    n_grp = grp_index.shape[0]
    pick = one_hot_rows(jnp.concatenate([dom_index, grp_index], axis=0), node_count)
    sent = jnp.dot(pick, features, preferred_element_type=jnp.float32).astype(jnp.bfloat16)
    table_bytes = n_dom * n_grp * bnd * (n_dom + n_grp) * bnd * 2
    if table_bytes <= PLACE_LIMIT:
        place, keep = placement(n_dom, n_grp, bnd)
        got = swap(sent, place, keep)
        recv_dom, recv_grp = got[: n_dom * bnd], got[n_dom * bnd :]
    else:
        sent = sent.reshape(n_dom + n_grp, bnd, width)
        recv_dom, recv_grp = exchange(sent[:n_dom], sent[n_dom:])
    source = jnp.concatenate(
        [features, recv_dom.reshape(-1, width), recv_grp.reshape(-1, width)], axis=0
    )
    source = source.reshape(-1, tile_size, width)
    source_count = source.shape[0]
    slot_count = tile_vals.shape[0]
    usable = jnp.arange(slot_count, dtype=jnp.int32) < tile_count[0]
    to_target = (
        (tile_tgt[None, :] == jnp.arange(block_count, dtype=jnp.int32)[:, None]) & usable[None, :]
    ).astype(jnp.float32)
    to_source = (
        (tile_src[None, :] == jnp.arange(source_count, dtype=jnp.int32)[:, None]) & usable[None, :]
    ).astype(jnp.float32)
    products = jnp.einsum(
        "tjf,tij->tfi", source[tile_src], tile_vals, preferred_element_type=jnp.float32
    )
    summed = jnp.einsum("bt,tfi->bif", to_target, products, precision=lax.Precision.HIGHEST)
    unit_column = jnp.ones((tile_size,), jnp.bfloat16)
    row_sums = jnp.einsum("tij,j->ti", tile_vals, unit_column, preferred_element_type=jnp.float32)
    degree = jnp.dot(to_target, row_sums, precision=lax.Precision.HIGHEST)
    agg = (summed / degree[:, :, None]).reshape(node_count, width).astype(jnp.bfloat16)
    preact = jnp.dot(features, w_self, preferred_element_type=jnp.float32) + jnp.dot(
        agg, w_neigh, preferred_element_type=jnp.float32
    )
    sigm = jax.nn.sigmoid(preact)
    output = (preact * sigm).astype(jnp.bfloat16)
    grad_pre = (cotangent.astype(jnp.float32) * sigm * (1.0 + preact * (1.0 - sigm))).astype(
        jnp.bfloat16
    )
    part_self = jnp.einsum("nf,nh->fh", features, grad_pre, preferred_element_type=jnp.float32)
    part_neigh = jnp.einsum("nf,nh->fh", agg, grad_pre, preferred_element_type=jnp.float32)
    grad_own = jnp.einsum("nh,fh->nf", grad_pre, w_self, preferred_element_type=jnp.float32)
    grad_agg = jnp.einsum("nh,fh->nf", grad_pre, w_neigh, preferred_element_type=jnp.float32)
    grad_agg = (grad_agg / degree.reshape(-1)[:, None]).astype(jnp.bfloat16)
    picked = grad_agg.reshape(block_count, tile_size, width)[tile_tgt]
    backward = jnp.einsum("tif,tij->tfj", picked, tile_vals, preferred_element_type=jnp.float32)
    grad_source = jnp.einsum(
        "st,tfj->sjf", to_source, backward, precision=lax.Precision.HIGHEST
    ).reshape(-1, width)
    remote = grad_source[node_count:].astype(jnp.bfloat16)
    if table_bytes <= PLACE_LIMIT:
        returned = swap(remote, place, keep)
    else:
        remote = remote.reshape(n_dom + n_grp, bnd, width)
        ret_dom, ret_grp = exchange(remote[:n_dom], remote[n_dom:])
        returned = jnp.concatenate([ret_dom.reshape(-1, width), ret_grp.reshape(-1, width)])
    grad_self, grad_neigh = weight_sum(part_self, part_neigh)
    grad_total = grad_own + grad_source[:node_count]
    grad_total = grad_total + lax.dot_general(
        pick, returned, (((0,), (0,)), ((), ())), preferred_element_type=jnp.float32
    )
    return (output, grad_total.astype(jnp.bfloat16), grad_self, grad_neigh)


def solution(mesh):
    return jax.shard_map(
        per_device,
        mesh=mesh,
        in_specs=(
            P(("dom", "grp"), None),
            P(("dom", "grp"), None, None),
            P(("dom", "grp"), None, None),
            P(("dom", "grp"), None, None),
            P(("dom", "grp")),
            P(("dom", "grp")),
            P(("dom", "grp")),
            P(),
            P(),
            P(("dom", "grp"), None),
        ),
        out_specs=(P(("dom", "grp"), None), P(("dom", "grp"), None), P(), P()),
        check_vma=False,
    )
```

```python
import jax
import jax.numpy as jnp
from jax import lax
from jax.sharding import PartitionSpec as P


def weight_sum(part_self, part_neigh, stacked=None):
    axes = ("dom", "grp")
    peers = lax.psum(1, axes)
    rows = part_self.shape[0]
    if stacked is None:
        stacked = jnp.concatenate([part_self, part_neigh], axis=0)
    if stacked.shape[0] % (8 * peers) == 0:
        chunks = stacked.reshape(peers, -1, stacked.shape[1])
        mine = jnp.sum(lax.all_to_all(chunks, axes, 0, 0, tiled=True), axis=0, keepdims=True)
        total = lax.all_to_all(jnp.broadcast_to(mine, chunks.shape), axes, 0, 0, tiled=True)
        total = total.reshape(stacked.shape)
        return total[:rows], total[rows:]
    flat = stacked.reshape(-1)
    pad = (-flat.shape[0]) % peers
    chunks = jnp.pad(flat, (0, pad)).reshape(peers, -1)
    mine = jnp.sum(lax.all_to_all(chunks, axes, 0, 0, tiled=True), axis=0, keepdims=True)
    spread = jnp.broadcast_to(mine, chunks.shape)
    total = lax.all_to_all(spread, axes, 0, 0, tiled=True).reshape(-1)
    total = total[: flat.shape[0]].reshape(stacked.shape)
    return total[:rows], total[rows:]


def exchange(dom_part, grp_part):
    axes = ("dom", "grp")
    n_dom, n_grp = dom_part.shape[0], grp_part.shape[0]
    a = lax.axis_index("dom")
    b = lax.axis_index("grp")
    cell = dom_part.shape[1:]
    buf = jnp.zeros((n_dom, n_grp) + cell, dom_part.dtype)
    buf = lax.dynamic_update_slice_in_dim(buf, dom_part[:, None], b, axis=1)
    buf = lax.dynamic_update_slice_in_dim(buf, grp_part[None], a, axis=0)
    got = lax.all_to_all(buf.reshape((n_dom * n_grp,) + cell), axes, 0, 0, tiled=True)
    got = got.reshape((n_dom, n_grp) + cell)
    from_dom = lax.dynamic_index_in_dim(got, b, axis=1, keepdims=False)
    own_dom = lax.dynamic_index_in_dim(dom_part, a, axis=0, keepdims=True)
    from_dom = lax.dynamic_update_slice_in_dim(from_dom, own_dom, a, axis=0)
    from_grp = lax.dynamic_index_in_dim(got, a, axis=0, keepdims=False)
    return from_dom, from_grp


def one_hot_rows(index, count):
    hot = index[..., None] == jnp.arange(count, dtype=jnp.int32)
    return hot.astype(jnp.bfloat16).reshape(-1, count)


PLACE_LIMIT = 4 << 20


def placement(n_dom, n_grp, bnd):
    a = lax.axis_index("dom")
    b = lax.axis_index("grp")
    blk = jnp.arange(n_dom + n_grp, dtype=jnp.int32)
    cell = jnp.where(blk < n_dom, blk * n_grp + b, a * n_grp + (blk - n_dom))
    local = blk == a
    cell = jnp.where(local, -1, cell)
    col = cell[:, None] * bnd + jnp.arange(bnd, dtype=jnp.int32)[None, :]
    place = one_hot_rows(col, n_dom * n_grp * bnd)
    keep = jnp.broadcast_to(local[:, None], (n_dom + n_grp, bnd)).reshape(-1, 1)
    return place, keep


def swap(table, place, keep):
    peers = lax.psum(1, ("dom", "grp"))
    buf = lax.dot_general(place, table, (((0,), (0,)), ((), ())), preferred_element_type=jnp.float32)
    buf = buf.astype(table.dtype).reshape(peers, -1, table.shape[1])
    got = lax.all_to_all(buf, ("dom", "grp"), 0, 0, tiled=True).reshape(-1, table.shape[1])
    back = jnp.dot(place, got, preferred_element_type=jnp.float32).astype(table.dtype)
    return jnp.where(keep, table, back)


def per_device(
    features,
    send_dom,
    send_grp,
    tile_vals,
    tile_tgt,
    tile_src,
    tile_count,
    w_self,
    w_neigh,
    cotangent,
):
    tile_size = tile_vals.shape[1]
    width = features.shape[1]
    node_count = features.shape[0]
    block_count = node_count // tile_size
    dom_index = send_dom[0]
    grp_index = send_grp[0]
    n_dom, bnd = dom_index.shape
    n_grp = grp_index.shape[0]
    pick = one_hot_rows(jnp.concatenate([dom_index, grp_index], axis=0), node_count)
    sent = jnp.dot(pick, features, preferred_element_type=jnp.float32).astype(jnp.bfloat16)
    table_bytes = n_dom * n_grp * bnd * (n_dom + n_grp) * bnd * 2
    if table_bytes <= PLACE_LIMIT:
        place, keep = placement(n_dom, n_grp, bnd)
        got = swap(sent, place, keep)
        recv_dom, recv_grp = got[: n_dom * bnd], got[n_dom * bnd :]
    else:
        sent = sent.reshape(n_dom + n_grp, bnd, width)
        recv_dom, recv_grp = exchange(sent[:n_dom], sent[n_dom:])
    source = jnp.concatenate(
        [features, recv_dom.reshape(-1, width), recv_grp.reshape(-1, width)], axis=0
    )
    source = source.reshape(-1, tile_size, width)
    source_count = source.shape[0]
    slot_count = tile_vals.shape[0]
    usable = jnp.arange(slot_count, dtype=jnp.int32) < tile_count[0]
    to_target = (
        (tile_tgt[None, :] == jnp.arange(block_count, dtype=jnp.int32)[:, None]) & usable[None, :]
    ).astype(jnp.float32)
    to_source = (
        (tile_src[None, :] == jnp.arange(source_count, dtype=jnp.int32)[:, None]) & usable[None, :]
    ).astype(jnp.float32)
    products = jnp.einsum(
        "tjf,tij->tfi", source[tile_src], tile_vals, preferred_element_type=jnp.float32
    )
    summed = jnp.einsum("bt,tfi->bif", to_target, products, precision=lax.Precision.HIGHEST)
    unit_column = jnp.ones((tile_size,), jnp.bfloat16)
    row_sums = jnp.einsum("tij,j->ti", tile_vals, unit_column, preferred_element_type=jnp.float32)
    degree = jnp.dot(to_target, row_sums, precision=lax.Precision.HIGHEST)
    agg = (summed / degree[:, :, None]).reshape(node_count, width).astype(jnp.bfloat16)
    preact = jnp.dot(features, w_self, preferred_element_type=jnp.float32) + jnp.dot(
        agg, w_neigh, preferred_element_type=jnp.float32
    )
    sigm = jax.nn.sigmoid(preact)
    output = (preact * sigm).astype(jnp.bfloat16)
    grad_pre = (cotangent.astype(jnp.float32) * sigm * (1.0 + preact * (1.0 - sigm))).astype(
        jnp.bfloat16
    )
    stacked = jnp.einsum(
        "nf,nh->fh", jnp.concatenate([features, agg], axis=1), grad_pre,
        preferred_element_type=jnp.float32,
    )
    part_self, part_neigh = stacked[:width], stacked[width:]
    grad_own = jnp.einsum("nh,fh->nf", grad_pre, w_self, preferred_element_type=jnp.float32)
    grad_agg = jnp.einsum("nh,fh->nf", grad_pre, w_neigh, preferred_element_type=jnp.float32)
    grad_agg = (grad_agg / degree.reshape(-1)[:, None]).astype(jnp.bfloat16)
    picked = grad_agg.reshape(block_count, tile_size, width)[tile_tgt]
    backward = jnp.einsum("tif,tij->tfj", picked, tile_vals, preferred_element_type=jnp.float32)
    grad_source = jnp.einsum(
        "st,tfj->sjf", to_source, backward, precision=lax.Precision.HIGHEST
    ).reshape(-1, width)
    remote = grad_source[node_count:].astype(jnp.bfloat16)
    if table_bytes <= PLACE_LIMIT:
        returned = swap(remote, place, keep)
    else:
        remote = remote.reshape(n_dom + n_grp, bnd, width)
        ret_dom, ret_grp = exchange(remote[:n_dom], remote[n_dom:])
        returned = jnp.concatenate([ret_dom.reshape(-1, width), ret_grp.reshape(-1, width)])
    grad_self, grad_neigh = weight_sum(part_self, part_neigh, stacked)
    grad_total = grad_own + grad_source[:node_count]
    grad_total = grad_total + lax.dot_general(
        pick, returned, (((0,), (0,)), ((), ())), preferred_element_type=jnp.float32
    )
    return (output, grad_total.astype(jnp.bfloat16), grad_self, grad_neigh)


def solution(mesh):
    return jax.shard_map(
        per_device,
        mesh=mesh,
        in_specs=(
            P(("dom", "grp"), None),
            P(("dom", "grp"), None, None),
            P(("dom", "grp"), None, None),
            P(("dom", "grp"), None, None),
            P(("dom", "grp")),
            P(("dom", "grp")),
            P(("dom", "grp")),
            P(),
            P(),
            P(("dom", "grp"), None),
        ),
        out_specs=(P(("dom", "grp"), None), P(("dom", "grp"), None), P(), P()),
        check_vma=False,
    )
```

```python
import jax
import jax.numpy as jnp
from jax import lax
from jax.sharding import PartitionSpec as P


def weight_sum(part_self, part_neigh):
    axes = ("dom", "grp")
    peers = lax.psum(1, axes)
    rows = part_self.shape[0]
    stacked = jnp.concatenate([part_self, part_neigh], axis=0)
    flat = stacked.reshape(-1)
    pad = (-flat.shape[0]) % peers
    chunks = jnp.pad(flat, (0, pad)).reshape(peers, -1)
    mine = jnp.sum(lax.all_to_all(chunks, axes, 0, 0, tiled=True), axis=0, keepdims=True)
    spread = jnp.broadcast_to(mine, chunks.shape)
    total = lax.all_to_all(spread, axes, 0, 0, tiled=True).reshape(-1)
    total = total[: flat.shape[0]].reshape(stacked.shape)
    return total[:rows], total[rows:]


def exchange(dom_part, grp_part):
    axes = ("dom", "grp")
    n_dom, n_grp = dom_part.shape[0], grp_part.shape[0]
    a = lax.axis_index("dom")
    b = lax.axis_index("grp")
    cell = dom_part.shape[1:]
    buf = jnp.zeros((n_dom, n_grp) + cell, dom_part.dtype)
    buf = lax.dynamic_update_slice_in_dim(buf, dom_part[:, None], b, axis=1)
    buf = lax.dynamic_update_slice_in_dim(buf, grp_part[None], a, axis=0)
    got = lax.all_to_all(buf.reshape((n_dom * n_grp,) + cell), axes, 0, 0, tiled=True)
    got = got.reshape((n_dom, n_grp) + cell)
    from_dom = lax.dynamic_index_in_dim(got, b, axis=1, keepdims=False)
    own_dom = lax.dynamic_index_in_dim(dom_part, a, axis=0, keepdims=True)
    from_dom = lax.dynamic_update_slice_in_dim(from_dom, own_dom, a, axis=0)
    from_grp = lax.dynamic_index_in_dim(got, a, axis=0, keepdims=False)
    return from_dom, from_grp


ADJ_LIMIT = 4 << 20


def split_bf16(value):
    hi = value.astype(jnp.bfloat16)
    rest = value - hi.astype(jnp.float32)
    mid = rest.astype(jnp.bfloat16)
    low = (rest - mid.astype(jnp.float32)).astype(jnp.bfloat16)
    return hi, mid, low


def one_hot_rows(index, count):
    hot = index[..., None] == jnp.arange(count, dtype=jnp.int32)
    return hot.astype(jnp.bfloat16).reshape(-1, count)


PLACE_LIMIT = 4 << 20


def placement(n_dom, n_grp, bnd):
    a = lax.axis_index("dom")
    b = lax.axis_index("grp")
    blk = jnp.arange(n_dom + n_grp, dtype=jnp.int32)
    cell = jnp.where(blk < n_dom, blk * n_grp + b, a * n_grp + (blk - n_dom))
    local = blk == a
    cell = jnp.where(local, -1, cell)
    col = cell[:, None] * bnd + jnp.arange(bnd, dtype=jnp.int32)[None, :]
    place = one_hot_rows(col, n_dom * n_grp * bnd)
    keep = jnp.broadcast_to(local[:, None], (n_dom + n_grp, bnd)).reshape(-1, 1)
    return place, keep


def swap(table, place, keep):
    peers = lax.psum(1, ("dom", "grp"))
    buf = lax.dot_general(place, table, (((0,), (0,)), ((), ())), preferred_element_type=jnp.float32)
    buf = buf.astype(table.dtype).reshape(peers, -1, table.shape[1])
    got = lax.all_to_all(buf, ("dom", "grp"), 0, 0, tiled=True).reshape(-1, table.shape[1])
    back = jnp.dot(place, got, preferred_element_type=jnp.float32).astype(table.dtype)
    return jnp.where(keep, table, back)


def per_device(
    features,
    send_dom,
    send_grp,
    tile_vals,
    tile_tgt,
    tile_src,
    tile_count,
    w_self,
    w_neigh,
    cotangent,
):
    tile_size = tile_vals.shape[1]
    width = features.shape[1]
    node_count = features.shape[0]
    block_count = node_count // tile_size
    dom_index = send_dom[0]
    grp_index = send_grp[0]
    n_dom, bnd = dom_index.shape
    n_grp = grp_index.shape[0]
    pick = one_hot_rows(jnp.concatenate([dom_index, grp_index], axis=0), node_count)
    sent = jnp.dot(pick, features, preferred_element_type=jnp.float32).astype(jnp.bfloat16)
    table_bytes = n_dom * n_grp * bnd * (n_dom + n_grp) * bnd * 2
    slot_count = tile_vals.shape[0]
    source_count = block_count + (n_dom + n_grp) * bnd // tile_size
    remote_count = source_count - block_count
    usable = jnp.arange(slot_count, dtype=jnp.int32) < tile_count[0]
    to_target = (
        (tile_tgt[None, :] == jnp.arange(block_count, dtype=jnp.int32)[:, None]) & usable[None, :]
    ).astype(jnp.float32)
    to_source = (
        (tile_src[None, :] == jnp.arange(source_count, dtype=jnp.int32)[:, None]) & usable[None, :]
    ).astype(jnp.float32)
    unit_column = jnp.ones((tile_size,), jnp.bfloat16)
    row_sums = jnp.einsum("tij,j->ti", tile_vals, unit_column, preferred_element_type=jnp.float32)
    degree = jnp.dot(to_target, row_sums, precision=lax.Precision.HIGHEST)
    split = table_bytes <= PLACE_LIMIT and (
        block_count * remote_count * tile_size * tile_size * 4 <= ADJ_LIMIT
    )
    if split:
        is_own = tile_src < block_count
        own_src = jnp.where(is_own, tile_src, 0)
        own_target = to_target * is_own.astype(jnp.float32)[None, :]
        remote_of = (
            tile_src[None, :] == block_count + jnp.arange(remote_count, dtype=jnp.int32)[:, None]
        ).astype(jnp.float32)
        pair = (to_target[:, None, :] * remote_of[None, :, :]).reshape(-1, slot_count)
        adj = jnp.dot(
            pair.astype(jnp.bfloat16), tile_vals.reshape(slot_count, -1),
            preferred_element_type=jnp.float32,
        )
        adj = adj.reshape(block_count, remote_count, tile_size, tile_size).transpose(0, 2, 1, 3)
        adj = adj.reshape(node_count, remote_count * tile_size)
        pieces = split_bf16(adj)
        own_blocks = features.reshape(block_count, tile_size, width)
        products = jnp.einsum(
            "tjf,tij->tfi", own_blocks[own_src], tile_vals, preferred_element_type=jnp.float32
        )
        summed = jnp.einsum("bt,tfi->bif", own_target, products, precision=lax.Precision.HIGHEST)
        place, keep = placement(n_dom, n_grp, bnd)
        received = swap(sent, place, keep)
        far = sum(jnp.dot(p, received, preferred_element_type=jnp.float32) for p in pieces)
        summed = summed.reshape(node_count, width) + far
    else:
        sent = sent.reshape(n_dom + n_grp, bnd, width)
        recv_dom, recv_grp = exchange(sent[:n_dom], sent[n_dom:])
        source = jnp.concatenate(
            [features, recv_dom.reshape(-1, width), recv_grp.reshape(-1, width)], axis=0
        )
        source = source.reshape(-1, tile_size, width)
        products = jnp.einsum(
            "tjf,tij->tfi", source[tile_src], tile_vals, preferred_element_type=jnp.float32
        )
        summed = jnp.einsum("bt,tfi->bif", to_target, products, precision=lax.Precision.HIGHEST)
        summed = summed.reshape(node_count, width)
    agg = (summed / degree.reshape(-1)[:, None]).astype(jnp.bfloat16)
    preact = jnp.dot(features, w_self, preferred_element_type=jnp.float32) + jnp.dot(
        agg, w_neigh, preferred_element_type=jnp.float32
    )
    sigm = jax.nn.sigmoid(preact)
    output = (preact * sigm).astype(jnp.bfloat16)
    grad_pre = (cotangent.astype(jnp.float32) * sigm * (1.0 + preact * (1.0 - sigm))).astype(
        jnp.bfloat16
    )
    part_self = jnp.einsum("nf,nh->fh", features, grad_pre, preferred_element_type=jnp.float32)
    part_neigh = jnp.einsum("nf,nh->fh", agg, grad_pre, preferred_element_type=jnp.float32)
    grad_own = jnp.einsum("nh,fh->nf", grad_pre, w_self, preferred_element_type=jnp.float32)
    grad_agg = jnp.einsum("nh,fh->nf", grad_pre, w_neigh, preferred_element_type=jnp.float32)
    grad_agg = (grad_agg / degree.reshape(-1)[:, None]).astype(jnp.bfloat16)
    picked = grad_agg.reshape(block_count, tile_size, width)[tile_tgt]
    backward = jnp.einsum("tif,tij->tfj", picked, tile_vals, preferred_element_type=jnp.float32)
    grad_source = jnp.einsum(
        "st,tfj->sjf", to_source, backward, precision=lax.Precision.HIGHEST
    ).reshape(-1, width)
    remote = grad_source[node_count:].astype(jnp.bfloat16)
    if split:
        returned = swap(remote, place, keep)
    else:
        remote = remote.reshape(n_dom + n_grp, bnd, width)
        ret_dom, ret_grp = exchange(remote[:n_dom], remote[n_dom:])
        returned = jnp.concatenate([ret_dom.reshape(-1, width), ret_grp.reshape(-1, width)])
    grad_self, grad_neigh = weight_sum(part_self, part_neigh)
    grad_total = grad_own + grad_source[:node_count]
    grad_total = grad_total + lax.dot_general(
        pick, returned, (((0,), (0,)), ((), ())), preferred_element_type=jnp.float32
    )
    return (output, grad_total.astype(jnp.bfloat16), grad_self, grad_neigh)


def solution(mesh):
    return jax.shard_map(
        per_device,
        mesh=mesh,
        in_specs=(
            P(("dom", "grp"), None),
            P(("dom", "grp"), None, None),
            P(("dom", "grp"), None, None),
            P(("dom", "grp"), None, None),
            P(("dom", "grp")),
            P(("dom", "grp")),
            P(("dom", "grp")),
            P(),
            P(),
            P(("dom", "grp"), None),
        ),
        out_specs=(P(("dom", "grp"), None), P(("dom", "grp"), None), P(), P()),
        check_vma=False,
    )
```

```python
import jax
import jax.numpy as jnp
from jax import lax
from jax.sharding import PartitionSpec as P


def weight_sum(part_self, part_neigh):
    axes = ("dom", "grp")
    peers = lax.psum(1, axes)
    rows = part_self.shape[0]
    stacked = jnp.concatenate([part_self, part_neigh], axis=0)
    flat = stacked.reshape(-1)
    pad = (-flat.shape[0]) % peers
    chunks = jnp.pad(flat, (0, pad)).reshape(peers, -1)
    mine = jnp.sum(lax.all_to_all(chunks, axes, 0, 0, tiled=True), axis=0, keepdims=True)
    spread = jnp.broadcast_to(mine, chunks.shape)
    total = lax.all_to_all(spread, axes, 0, 0, tiled=True).reshape(-1)
    total = total[: flat.shape[0]].reshape(stacked.shape)
    return total[:rows], total[rows:]


def exchange(dom_part, grp_part):
    axes = ("dom", "grp")
    n_dom, n_grp = dom_part.shape[0], grp_part.shape[0]
    a = lax.axis_index("dom")
    b = lax.axis_index("grp")
    cell = dom_part.shape[1:]
    buf = jnp.zeros((n_dom, n_grp) + cell, dom_part.dtype)
    buf = lax.dynamic_update_slice_in_dim(buf, dom_part[:, None], b, axis=1)
    buf = lax.dynamic_update_slice_in_dim(buf, grp_part[None], a, axis=0)
    got = lax.all_to_all(buf.reshape((n_dom * n_grp,) + cell), axes, 0, 0, tiled=True)
    got = got.reshape((n_dom, n_grp) + cell)
    from_dom = lax.dynamic_index_in_dim(got, b, axis=1, keepdims=False)
    own_dom = lax.dynamic_index_in_dim(dom_part, a, axis=0, keepdims=True)
    from_dom = lax.dynamic_update_slice_in_dim(from_dom, own_dom, a, axis=0)
    from_grp = lax.dynamic_index_in_dim(got, a, axis=0, keepdims=False)
    return from_dom, from_grp


def one_hot_rows(index, count):
    hot = index[..., None] == jnp.arange(count, dtype=jnp.int32)
    return hot.astype(jnp.bfloat16).reshape(-1, count)


PLACE_LIMIT = 4 << 20


def placement(n_dom, n_grp, bnd):
    a = lax.axis_index("dom")
    b = lax.axis_index("grp")
    blk = jnp.arange(n_dom + n_grp, dtype=jnp.int32)
    cell = jnp.where(blk < n_dom, blk * n_grp + b, a * n_grp + (blk - n_dom))
    local = blk == a
    cell = jnp.where(local, -1, cell)
    col = cell[:, None] * bnd + jnp.arange(bnd, dtype=jnp.int32)[None, :]
    place = one_hot_rows(col, n_dom * n_grp * bnd)
    keep = jnp.broadcast_to(local[:, None], (n_dom + n_grp, bnd)).reshape(-1, 1)
    return place, keep


def swap(table, place, keep):
    peers = lax.psum(1, ("dom", "grp"))
    buf = lax.dot_general(place, table, (((0,), (0,)), ((), ())), preferred_element_type=jnp.float32)
    buf = buf.astype(table.dtype).reshape(peers, -1, table.shape[1])
    got = lax.all_to_all(buf, ("dom", "grp"), 0, 0, tiled=True).reshape(-1, table.shape[1])
    back = jnp.dot(place, got, preferred_element_type=jnp.float32).astype(table.dtype)
    return jnp.where(keep, table, back)


def per_device(
    features,
    send_dom,
    send_grp,
    tile_vals,
    tile_tgt,
    tile_src,
    tile_count,
    w_self,
    w_neigh,
    cotangent,
):
    tile_size = tile_vals.shape[1]
    width = features.shape[1]
    node_count = features.shape[0]
    block_count = node_count // tile_size
    dom_index = send_dom[0]
    grp_index = send_grp[0]
    n_dom, bnd = dom_index.shape
    n_grp = grp_index.shape[0]
    pick = one_hot_rows(jnp.concatenate([dom_index, grp_index], axis=0), node_count)
    sent = jnp.dot(pick, features, preferred_element_type=jnp.float32).astype(jnp.bfloat16)
    table_bytes = n_dom * n_grp * bnd * (n_dom + n_grp) * bnd * 2
    if table_bytes <= PLACE_LIMIT:
        place, keep = placement(n_dom, n_grp, bnd)
        got = swap(sent, place, keep)
        recv_dom, recv_grp = got[: n_dom * bnd], got[n_dom * bnd :]
    else:
        sent = sent.reshape(n_dom + n_grp, bnd, width)
        recv_dom, recv_grp = exchange(sent[:n_dom], sent[n_dom:])
    source = jnp.concatenate(
        [features, recv_dom.reshape(-1, width), recv_grp.reshape(-1, width)], axis=0
    )
    source = source.reshape(-1, tile_size, width)
    source_count = source.shape[0]
    slot_count = tile_vals.shape[0]
    usable = jnp.arange(slot_count, dtype=jnp.int32) < tile_count[0]
    to_target = (
        (tile_tgt[None, :] == jnp.arange(block_count, dtype=jnp.int32)[:, None]) & usable[None, :]
    ).astype(jnp.float32)
    to_source = (
        (tile_src[None, :] == jnp.arange(source_count, dtype=jnp.int32)[:, None]) & usable[None, :]
    ).astype(jnp.float32)
    products = jnp.einsum(
        "tjf,tij->tfi", source[tile_src], tile_vals, preferred_element_type=jnp.float32
    )
    summed = jnp.einsum("bt,tfi->bif", to_target, products, precision=lax.Precision.HIGH)
    unit_column = jnp.ones((tile_size,), jnp.bfloat16)
    row_sums = jnp.einsum("tij,j->ti", tile_vals, unit_column, preferred_element_type=jnp.float32)
    degree = jnp.dot(to_target, row_sums, precision=lax.Precision.HIGHEST)
    agg = (summed / degree[:, :, None]).reshape(node_count, width).astype(jnp.bfloat16)
    preact = jnp.dot(features, w_self, preferred_element_type=jnp.float32) + jnp.dot(
        agg, w_neigh, preferred_element_type=jnp.float32
    )
    sigm = jax.nn.sigmoid(preact)
    output = (preact * sigm).astype(jnp.bfloat16)
    grad_pre = (cotangent.astype(jnp.float32) * sigm * (1.0 + preact * (1.0 - sigm))).astype(
        jnp.bfloat16
    )
    part_self = jnp.einsum("nf,nh->fh", features, grad_pre, preferred_element_type=jnp.float32)
    part_neigh = jnp.einsum("nf,nh->fh", agg, grad_pre, preferred_element_type=jnp.float32)
    grad_own = jnp.einsum("nh,fh->nf", grad_pre, w_self, preferred_element_type=jnp.float32)
    grad_agg = jnp.einsum("nh,fh->nf", grad_pre, w_neigh, preferred_element_type=jnp.float32)
    grad_agg = (grad_agg / degree.reshape(-1)[:, None]).astype(jnp.bfloat16)
    picked = grad_agg.reshape(block_count, tile_size, width)[tile_tgt]
    backward = jnp.einsum("tif,tij->tfj", picked, tile_vals, preferred_element_type=jnp.float32)
    grad_source = jnp.einsum(
        "st,tfj->sjf", to_source, backward, precision=lax.Precision.HIGH
    ).reshape(-1, width)
    remote = grad_source[node_count:].astype(jnp.bfloat16)
    if table_bytes <= PLACE_LIMIT:
        returned = swap(remote, place, keep)
    else:
        remote = remote.reshape(n_dom + n_grp, bnd, width)
        ret_dom, ret_grp = exchange(remote[:n_dom], remote[n_dom:])
        returned = jnp.concatenate([ret_dom.reshape(-1, width), ret_grp.reshape(-1, width)])
    grad_self, grad_neigh = weight_sum(part_self, part_neigh)
    grad_total = grad_own + grad_source[:node_count]
    grad_total = grad_total + lax.dot_general(
        pick, returned, (((0,), (0,)), ((), ())), preferred_element_type=jnp.float32
    )
    return (output, grad_total.astype(jnp.bfloat16), grad_self, grad_neigh)


def solution(mesh):
    return jax.shard_map(
        per_device,
        mesh=mesh,
        in_specs=(
            P(("dom", "grp"), None),
            P(("dom", "grp"), None, None),
            P(("dom", "grp"), None, None),
            P(("dom", "grp"), None, None),
            P(("dom", "grp")),
            P(("dom", "grp")),
            P(("dom", "grp")),
            P(),
            P(),
            P(("dom", "grp"), None),
        ),
        out_specs=(P(("dom", "grp"), None), P(("dom", "grp"), None), P(), P()),
        check_vma=False,
    )
```

```python
import jax
import jax.numpy as jnp
from jax import lax
from jax.sharding import PartitionSpec as P


def weight_sum(part_self, part_neigh, stacked=None):
    axes = ("dom", "grp")
    peers = lax.psum(1, axes)
    rows = part_self.shape[0]
    if stacked is None:
        stacked = jnp.concatenate([part_self, part_neigh], axis=0)
    if stacked.shape[0] % (8 * peers) == 0:
        chunks = stacked.reshape(peers, -1, stacked.shape[1])
        mine = jnp.sum(lax.all_to_all(chunks, axes, 0, 0, tiled=True), axis=0, keepdims=True)
        total = lax.all_to_all(jnp.broadcast_to(mine, chunks.shape), axes, 0, 0, tiled=True)
        total = total.reshape(stacked.shape)
        return total[:rows], total[rows:]
    flat = stacked.reshape(-1)
    pad = (-flat.shape[0]) % peers
    chunks = jnp.pad(flat, (0, pad)).reshape(peers, -1)
    mine = jnp.sum(lax.all_to_all(chunks, axes, 0, 0, tiled=True), axis=0, keepdims=True)
    spread = jnp.broadcast_to(mine, chunks.shape)
    total = lax.all_to_all(spread, axes, 0, 0, tiled=True).reshape(-1)
    total = total[: flat.shape[0]].reshape(stacked.shape)
    return total[:rows], total[rows:]


def exchange(dom_part, grp_part):
    axes = ("dom", "grp")
    n_dom, n_grp = dom_part.shape[0], grp_part.shape[0]
    a = lax.axis_index("dom")
    b = lax.axis_index("grp")
    cell = dom_part.shape[1:]
    buf = jnp.zeros((n_dom, n_grp) + cell, dom_part.dtype)
    buf = lax.dynamic_update_slice_in_dim(buf, dom_part[:, None], b, axis=1)
    buf = lax.dynamic_update_slice_in_dim(buf, grp_part[None], a, axis=0)
    got = lax.all_to_all(buf.reshape((n_dom * n_grp,) + cell), axes, 0, 0, tiled=True)
    got = got.reshape((n_dom, n_grp) + cell)
    from_dom = lax.dynamic_index_in_dim(got, b, axis=1, keepdims=False)
    own_dom = lax.dynamic_index_in_dim(dom_part, a, axis=0, keepdims=True)
    from_dom = lax.dynamic_update_slice_in_dim(from_dom, own_dom, a, axis=0)
    from_grp = lax.dynamic_index_in_dim(got, a, axis=0, keepdims=False)
    return from_dom, from_grp


def one_hot_rows(index, count):
    hot = index[..., None] == jnp.arange(count, dtype=jnp.int32)
    return hot.astype(jnp.bfloat16).reshape(-1, count)


PLACE_LIMIT = 4 << 20


def placement(n_dom, n_grp, bnd):
    a = lax.axis_index("dom")
    b = lax.axis_index("grp")
    blk = jnp.arange(n_dom + n_grp, dtype=jnp.int32)
    cell = jnp.where(blk < n_dom, blk * n_grp + b, a * n_grp + (blk - n_dom))
    local = blk == a
    cell = jnp.where(local, -1, cell)
    col = cell[:, None] * bnd + jnp.arange(bnd, dtype=jnp.int32)[None, :]
    place = one_hot_rows(col, n_dom * n_grp * bnd)
    keep = jnp.broadcast_to(local[:, None], (n_dom + n_grp, bnd)).reshape(-1, 1)
    return place, keep


def swap(table, place, keep):
    peers = lax.psum(1, ("dom", "grp"))
    buf = lax.dot_general(place, table, (((0,), (0,)), ((), ())), preferred_element_type=jnp.float32)
    buf = buf.astype(table.dtype).reshape(peers, -1, table.shape[1])
    got = lax.all_to_all(buf, ("dom", "grp"), 0, 0, tiled=True).reshape(-1, table.shape[1])
    back = jnp.dot(place, got, preferred_element_type=jnp.float32).astype(table.dtype)
    return jnp.where(keep, table, back)


def per_device(
    features,
    send_dom,
    send_grp,
    tile_vals,
    tile_tgt,
    tile_src,
    tile_count,
    w_self,
    w_neigh,
    cotangent,
):
    tile_size = tile_vals.shape[1]
    width = features.shape[1]
    node_count = features.shape[0]
    block_count = node_count // tile_size
    dom_index = send_dom[0]
    grp_index = send_grp[0]
    n_dom, bnd = dom_index.shape
    n_grp = grp_index.shape[0]
    pick = one_hot_rows(jnp.concatenate([dom_index, grp_index], axis=0), node_count)
    sent = jnp.dot(pick, features, preferred_element_type=jnp.float32).astype(jnp.bfloat16)
    table_bytes = n_dom * n_grp * bnd * (n_dom + n_grp) * bnd * 2
    if table_bytes <= PLACE_LIMIT:
        place, keep = placement(n_dom, n_grp, bnd)
        got = swap(sent, place, keep)
        recv_dom, recv_grp = got[: n_dom * bnd], got[n_dom * bnd :]
    else:
        sent = sent.reshape(n_dom + n_grp, bnd, width)
        recv_dom, recv_grp = exchange(sent[:n_dom], sent[n_dom:])
    source = jnp.concatenate(
        [features, recv_dom.reshape(-1, width), recv_grp.reshape(-1, width)], axis=0
    )
    source = source.reshape(-1, tile_size, width)
    source_count = source.shape[0]
    slot_count = tile_vals.shape[0]
    usable = jnp.arange(slot_count, dtype=jnp.int32) < tile_count[0]
    to_target = (
        (tile_tgt[None, :] == jnp.arange(block_count, dtype=jnp.int32)[:, None]) & usable[None, :]
    ).astype(jnp.float32)
    to_source = (
        (tile_src[None, :] == jnp.arange(source_count, dtype=jnp.int32)[:, None]) & usable[None, :]
    ).astype(jnp.float32)
    products = jnp.einsum(
        "tjf,tij->tfi", source[tile_src], tile_vals, preferred_element_type=jnp.float32
    )
    summed = jnp.einsum("bt,tfi->bif", to_target, products, precision=lax.Precision.HIGHEST)
    unit_column = jnp.ones((tile_size,), jnp.bfloat16)
    row_sums = jnp.einsum("tij,j->ti", tile_vals, unit_column, preferred_element_type=jnp.float32)
    degree = jnp.dot(to_target, row_sums, precision=lax.Precision.HIGHEST)
    agg = (summed / degree[:, :, None]).reshape(node_count, width).astype(jnp.bfloat16)
    preact = jnp.dot(features, w_self, preferred_element_type=jnp.float32) + jnp.dot(
        agg, w_neigh, preferred_element_type=jnp.float32
    )
    sigm = jax.nn.sigmoid(preact)
    output = (preact * sigm).astype(jnp.bfloat16)
    grad_pre = (cotangent.astype(jnp.float32) * sigm * (1.0 + preact * (1.0 - sigm))).astype(
        jnp.bfloat16
    )
    part_self = jnp.einsum("nf,nh->fh", features, grad_pre, preferred_element_type=jnp.float32)
    part_neigh = jnp.einsum("nf,nh->fh", agg, grad_pre, preferred_element_type=jnp.float32)
    grad_own = jnp.einsum("nh,fh->nf", grad_pre, w_self, preferred_element_type=jnp.float32)
    grad_agg = jnp.einsum("nh,fh->nf", grad_pre, w_neigh, preferred_element_type=jnp.float32)
    grad_agg = (grad_agg / degree.reshape(-1)[:, None]).astype(jnp.bfloat16)
    picked = grad_agg.reshape(block_count, tile_size, width)[tile_tgt]
    backward = jnp.einsum("tif,tij->tfj", picked, tile_vals, preferred_element_type=jnp.float32)
    grad_source = jnp.einsum(
        "st,tfj->sjf", to_source, backward, precision=lax.Precision.HIGHEST
    ).reshape(-1, width)
    remote = grad_source[node_count:].astype(jnp.bfloat16)
    if table_bytes <= PLACE_LIMIT:
        returned = swap(remote, place, keep)
    else:
        remote = remote.reshape(n_dom + n_grp, bnd, width)
        ret_dom, ret_grp = exchange(remote[:n_dom], remote[n_dom:])
        returned = jnp.concatenate([ret_dom.reshape(-1, width), ret_grp.reshape(-1, width)])
    grad_self, grad_neigh = weight_sum(part_self, part_neigh)
    grad_total = grad_own + grad_source[:node_count]
    grad_total = grad_total + lax.dot_general(
        pick, returned, (((0,), (0,)), ((), ())), preferred_element_type=jnp.float32
    )
    return (output, grad_total.astype(jnp.bfloat16), grad_self, grad_neigh)


def solution(mesh):
    return jax.shard_map(
        per_device,
        mesh=mesh,
        in_specs=(
            P(("dom", "grp"), None),
            P(("dom", "grp"), None, None),
            P(("dom", "grp"), None, None),
            P(("dom", "grp"), None, None),
            P(("dom", "grp")),
            P(("dom", "grp")),
            P(("dom", "grp")),
            P(),
            P(),
            P(("dom", "grp"), None),
        ),
        out_specs=(P(("dom", "grp"), None), P(("dom", "grp"), None), P(), P()),
        check_vma=False,
    )
```

```python
import jax
import jax.numpy as jnp
from jax import lax
from jax.sharding import PartitionSpec as P


def weight_sum(part_self, part_neigh, stacked=None):
    axes = ("dom", "grp")
    peers = lax.psum(1, axes)
    rows = part_self.shape[0]
    if stacked is None:
        stacked = jnp.concatenate([part_self, part_neigh], axis=0)
    if stacked.shape[0] % (8 * peers) == 0:
        chunks = stacked.reshape(peers, -1, stacked.shape[1])
        mine = jnp.sum(lax.all_to_all(chunks, axes, 0, 0, tiled=True), axis=0, keepdims=True)
        total = lax.all_to_all(jnp.broadcast_to(mine, chunks.shape), axes, 0, 0, tiled=True)
        total = total.reshape(stacked.shape)
        return total[:rows], total[rows:]
    flat = stacked.reshape(-1)
    pad = (-flat.shape[0]) % peers
    chunks = jnp.pad(flat, (0, pad)).reshape(peers, -1)
    mine = jnp.sum(lax.all_to_all(chunks, axes, 0, 0, tiled=True), axis=0, keepdims=True)
    spread = jnp.broadcast_to(mine, chunks.shape)
    total = lax.all_to_all(spread, axes, 0, 0, tiled=True).reshape(-1)
    total = total[: flat.shape[0]].reshape(stacked.shape)
    return total[:rows], total[rows:]


def exchange(dom_part, grp_part):
    axes = ("dom", "grp")
    n_dom, n_grp = dom_part.shape[0], grp_part.shape[0]
    a = lax.axis_index("dom")
    b = lax.axis_index("grp")
    cell = dom_part.shape[1:]
    buf = jnp.zeros((n_dom, n_grp) + cell, dom_part.dtype)
    buf = lax.dynamic_update_slice_in_dim(buf, dom_part[:, None], b, axis=1)
    buf = lax.dynamic_update_slice_in_dim(buf, grp_part[None], a, axis=0)
    got = lax.all_to_all(buf.reshape((n_dom * n_grp,) + cell), axes, 0, 0, tiled=True)
    got = got.reshape((n_dom, n_grp) + cell)
    from_dom = lax.dynamic_index_in_dim(got, b, axis=1, keepdims=False)
    own_dom = lax.dynamic_index_in_dim(dom_part, a, axis=0, keepdims=True)
    from_dom = lax.dynamic_update_slice_in_dim(from_dom, own_dom, a, axis=0)
    from_grp = lax.dynamic_index_in_dim(got, a, axis=0, keepdims=False)
    return from_dom, from_grp


def one_hot_rows(index, count):
    hot = index[..., None] == jnp.arange(count, dtype=jnp.int32)
    return hot.astype(jnp.bfloat16).reshape(-1, count)


PLACE_LIMIT = 4 << 20


def placement(n_dom, n_grp, bnd):
    a = lax.axis_index("dom")
    b = lax.axis_index("grp")
    blk = jnp.arange(n_dom + n_grp, dtype=jnp.int32)
    cell = jnp.where(blk < n_dom, blk * n_grp + b, a * n_grp + (blk - n_dom))
    local = blk == a
    cell = jnp.where(local, -1, cell)
    col = cell[:, None] * bnd + jnp.arange(bnd, dtype=jnp.int32)[None, :]
    place = one_hot_rows(col, n_dom * n_grp * bnd)
    keep = jnp.broadcast_to(local[:, None], (n_dom + n_grp, bnd)).reshape(-1, 1)
    return place, keep


def swap(table, place, keep):
    peers = lax.psum(1, ("dom", "grp"))
    buf = lax.dot_general(place, table, (((0,), (0,)), ((), ())), preferred_element_type=jnp.float32)
    buf = buf.astype(table.dtype).reshape(peers, -1, table.shape[1])
    got = lax.all_to_all(buf, ("dom", "grp"), 0, 0, tiled=True).reshape(-1, table.shape[1])
    back = jnp.dot(place, got, preferred_element_type=jnp.float32).astype(table.dtype)
    return jnp.where(keep, table, back)


def per_device(
    features,
    send_dom,
    send_grp,
    tile_vals,
    tile_tgt,
    tile_src,
    tile_count,
    w_self,
    w_neigh,
    cotangent,
):
    tile_size = tile_vals.shape[1]
    width = features.shape[1]
    node_count = features.shape[0]
    block_count = node_count // tile_size
    dom_index = send_dom[0]
    grp_index = send_grp[0]
    n_dom, bnd = dom_index.shape
    n_grp = grp_index.shape[0]
    pick = one_hot_rows(jnp.concatenate([dom_index, grp_index], axis=0), node_count)
    sent = jnp.dot(pick, features, preferred_element_type=jnp.float32).astype(jnp.bfloat16)
    table_bytes = n_dom * n_grp * bnd * (n_dom + n_grp) * bnd * 2
    if table_bytes <= PLACE_LIMIT:
        place, keep = placement(n_dom, n_grp, bnd)
        got = swap(sent, place, keep)
        recv_dom, recv_grp = got[: n_dom * bnd], got[n_dom * bnd :]
    else:
        sent = sent.reshape(n_dom + n_grp, bnd, width)
        recv_dom, recv_grp = exchange(sent[:n_dom], sent[n_dom:])
    source = jnp.concatenate(
        [features, recv_dom.reshape(-1, width), recv_grp.reshape(-1, width)], axis=0
    )
    source = source.reshape(-1, tile_size, width)
    source_count = source.shape[0]
    slot_count = tile_vals.shape[0]
    usable = jnp.arange(slot_count, dtype=jnp.int32) < tile_count[0]
    to_target = (
        (tile_tgt[None, :] == jnp.arange(block_count, dtype=jnp.int32)[:, None]) & usable[None, :]
    ).astype(jnp.float32)
    to_source = (
        (tile_src[None, :] == jnp.arange(source_count, dtype=jnp.int32)[:, None]) & usable[None, :]
    ).astype(jnp.float32)
    products = jnp.einsum(
        "tjf,tij->tfi", source[tile_src], tile_vals, preferred_element_type=jnp.float32
    )
    summed = jnp.einsum("bt,tfi->bif", to_target, products, precision=lax.Precision.HIGHEST)
    unit_column = jnp.ones((tile_size,), jnp.bfloat16)
    row_sums = jnp.einsum("tij,j->ti", tile_vals, unit_column, preferred_element_type=jnp.float32)
    degree = jnp.dot(to_target, row_sums, precision=lax.Precision.HIGHEST)
    agg = (summed / degree[:, :, None]).reshape(node_count, width).astype(jnp.bfloat16)
    preact = jnp.dot(features, w_self, preferred_element_type=jnp.float32) + jnp.dot(
        agg, w_neigh, preferred_element_type=jnp.float32
    )
    sigm = jax.nn.sigmoid(preact)
    output = (preact * sigm).astype(jnp.bfloat16)
    grad_pre = (cotangent.astype(jnp.float32) * sigm * (1.0 + preact * (1.0 - sigm))).astype(
        jnp.bfloat16
    )
    part_self = jnp.einsum("nf,nh->fh", features, grad_pre, preferred_element_type=jnp.float32)
    part_neigh = jnp.einsum("nf,nh->fh", agg, grad_pre, preferred_element_type=jnp.float32)
    grad_own = jnp.einsum("nh,fh->nf", grad_pre, w_self, preferred_element_type=jnp.float32)
    grad_agg = jnp.einsum("nh,fh->nf", grad_pre, w_neigh, preferred_element_type=jnp.float32)
    grad_agg = (grad_agg / degree.reshape(-1)[:, None]).astype(jnp.bfloat16)
    picked = grad_agg.reshape(block_count, tile_size, width)[tile_tgt]
    backward = jnp.einsum("tif,tij->tfj", picked, tile_vals, preferred_element_type=jnp.float32)
    grad_source = jnp.einsum("st,tfj->sfj", to_source, backward, precision=lax.Precision.HIGHEST)
    remote = grad_source[block_count:].transpose(0, 2, 1).reshape(-1, width).astype(jnp.bfloat16)
    if table_bytes <= PLACE_LIMIT:
        returned = swap(remote, place, keep)
    else:
        remote = remote.reshape(n_dom + n_grp, bnd, width)
        ret_dom, ret_grp = exchange(remote[:n_dom], remote[n_dom:])
        returned = jnp.concatenate([ret_dom.reshape(-1, width), ret_grp.reshape(-1, width)])
    grad_self, grad_neigh = weight_sum(part_self, part_neigh)
    grad_total = grad_own + grad_source[:block_count].transpose(0, 2, 1).reshape(node_count, width)
    grad_total = grad_total + lax.dot_general(
        pick, returned, (((0,), (0,)), ((), ())), preferred_element_type=jnp.float32
    )
    return (output, grad_total.astype(jnp.bfloat16), grad_self, grad_neigh)


def solution(mesh):
    return jax.shard_map(
        per_device,
        mesh=mesh,
        in_specs=(
            P(("dom", "grp"), None),
            P(("dom", "grp"), None, None),
            P(("dom", "grp"), None, None),
            P(("dom", "grp"), None, None),
            P(("dom", "grp")),
            P(("dom", "grp")),
            P(("dom", "grp")),
            P(),
            P(),
            P(("dom", "grp"), None),
        ),
        out_specs=(P(("dom", "grp"), None), P(("dom", "grp"), None), P(), P()),
        check_vma=False,
    )
```

```python
import jax
import jax.numpy as jnp
from jax import lax
from jax.sharding import PartitionSpec as P


def weight_sum(part_self, part_neigh, stacked=None):
    axes = ("dom", "grp")
    peers = lax.psum(1, axes)
    rows = part_self.shape[0]
    if stacked is None:
        stacked = jnp.concatenate([part_self, part_neigh], axis=0)
    if stacked.shape[0] % (8 * peers) == 0:
        chunks = stacked.reshape(peers, -1, stacked.shape[1])
        mine = jnp.sum(lax.all_to_all(chunks, axes, 0, 0, tiled=True), axis=0, keepdims=True)
        total = lax.all_to_all(jnp.broadcast_to(mine, chunks.shape), axes, 0, 0, tiled=True)
        total = total.reshape(stacked.shape)
        return total[:rows], total[rows:]
    flat = stacked.reshape(-1)
    pad = (-flat.shape[0]) % peers
    chunks = jnp.pad(flat, (0, pad)).reshape(peers, -1)
    mine = jnp.sum(lax.all_to_all(chunks, axes, 0, 0, tiled=True), axis=0, keepdims=True)
    spread = jnp.broadcast_to(mine, chunks.shape)
    total = lax.all_to_all(spread, axes, 0, 0, tiled=True).reshape(-1)
    total = total[: flat.shape[0]].reshape(stacked.shape)
    return total[:rows], total[rows:]


def exchange(dom_part, grp_part):
    axes = ("dom", "grp")
    n_dom, n_grp = dom_part.shape[0], grp_part.shape[0]
    a = lax.axis_index("dom")
    b = lax.axis_index("grp")
    cell = dom_part.shape[1:]
    buf = jnp.zeros((n_dom, n_grp) + cell, dom_part.dtype)
    buf = lax.dynamic_update_slice_in_dim(buf, dom_part[:, None], b, axis=1)
    buf = lax.dynamic_update_slice_in_dim(buf, grp_part[None], a, axis=0)
    got = lax.all_to_all(buf.reshape((n_dom * n_grp,) + cell), axes, 0, 0, tiled=True)
    got = got.reshape((n_dom, n_grp) + cell)
    from_dom = lax.dynamic_index_in_dim(got, b, axis=1, keepdims=False)
    own_dom = lax.dynamic_index_in_dim(dom_part, a, axis=0, keepdims=True)
    from_dom = lax.dynamic_update_slice_in_dim(from_dom, own_dom, a, axis=0)
    from_grp = lax.dynamic_index_in_dim(got, a, axis=0, keepdims=False)
    return from_dom, from_grp


def one_hot_rows(index, count):
    hot = index[..., None] == jnp.arange(count, dtype=jnp.int32)
    return hot.astype(jnp.bfloat16).reshape(-1, count)


PLACE_LIMIT = 4 << 20


def placement(n_dom, n_grp, bnd):
    a = lax.axis_index("dom")
    b = lax.axis_index("grp")
    blk = jnp.arange(n_dom + n_grp, dtype=jnp.int32)
    cell = jnp.where(blk < n_dom, blk * n_grp + b, a * n_grp + (blk - n_dom))
    local = blk == a
    cell = jnp.where(local, -1, cell)
    col = cell[:, None] * bnd + jnp.arange(bnd, dtype=jnp.int32)[None, :]
    place = one_hot_rows(col, n_dom * n_grp * bnd)
    keep = jnp.broadcast_to(local[:, None], (n_dom + n_grp, bnd)).reshape(-1, 1)
    return place, keep


def swap(table, place, keep):
    peers = lax.psum(1, ("dom", "grp"))
    buf = lax.dot_general(place, table, (((0,), (0,)), ((), ())), preferred_element_type=jnp.float32)
    buf = buf.astype(table.dtype).reshape(peers, -1, table.shape[1])
    got = lax.all_to_all(buf, ("dom", "grp"), 0, 0, tiled=True).reshape(-1, table.shape[1])
    back = jnp.dot(place, got, preferred_element_type=jnp.float32).astype(table.dtype)
    return jnp.where(keep, table, back)


def per_device(
    features,
    send_dom,
    send_grp,
    tile_vals,
    tile_tgt,
    tile_src,
    tile_count,
    w_self,
    w_neigh,
    cotangent,
):
    tile_size = tile_vals.shape[1]
    width = features.shape[1]
    node_count = features.shape[0]
    block_count = node_count // tile_size
    dom_index = send_dom[0]
    grp_index = send_grp[0]
    n_dom, bnd = dom_index.shape
    n_grp = grp_index.shape[0]
    pick = one_hot_rows(jnp.concatenate([dom_index, grp_index], axis=0), node_count)
    sent = jnp.dot(pick, features, preferred_element_type=jnp.float32).astype(jnp.bfloat16)
    table_bytes = n_dom * n_grp * bnd * (n_dom + n_grp) * bnd * 2
    if table_bytes <= PLACE_LIMIT:
        place, keep = placement(n_dom, n_grp, bnd)
        got = swap(sent, place, keep)
        recv_dom, recv_grp = got[: n_dom * bnd], got[n_dom * bnd :]
    else:
        sent = sent.reshape(n_dom + n_grp, bnd, width)
        recv_dom, recv_grp = exchange(sent[:n_dom], sent[n_dom:])
    source = jnp.concatenate(
        [features, recv_dom.reshape(-1, width), recv_grp.reshape(-1, width)], axis=0
    )
    source = source.reshape(-1, tile_size, width)
    source_count = source.shape[0]
    own_blocks = features.reshape(block_count, tile_size, width)
    far_blocks = source[block_count:]
    is_own = (tile_src < block_count)[:, None, None]
    gathered = jnp.where(
        is_own,
        own_blocks[jnp.clip(tile_src, 0, block_count - 1)],
        far_blocks[jnp.clip(tile_src - block_count, 0, source_count - block_count - 1)],
    )
    slot_count = tile_vals.shape[0]
    usable = jnp.arange(slot_count, dtype=jnp.int32) < tile_count[0]
    to_target = (
        (tile_tgt[None, :] == jnp.arange(block_count, dtype=jnp.int32)[:, None]) & usable[None, :]
    ).astype(jnp.float32)
    to_source = (
        (tile_src[None, :] == jnp.arange(source_count, dtype=jnp.int32)[:, None]) & usable[None, :]
    ).astype(jnp.float32)
    products = jnp.einsum(
        "tjf,tij->tfi", gathered, tile_vals, preferred_element_type=jnp.float32
    )
    summed = jnp.einsum("bt,tfi->bif", to_target, products, precision=lax.Precision.HIGHEST)
    unit_column = jnp.ones((tile_size,), jnp.bfloat16)
    row_sums = jnp.einsum("tij,j->ti", tile_vals, unit_column, preferred_element_type=jnp.float32)
    degree = jnp.dot(to_target, row_sums, precision=lax.Precision.HIGHEST)
    agg = (summed / degree[:, :, None]).reshape(node_count, width).astype(jnp.bfloat16)
    preact = jnp.dot(features, w_self, preferred_element_type=jnp.float32) + jnp.dot(
        agg, w_neigh, preferred_element_type=jnp.float32
    )
    sigm = jax.nn.sigmoid(preact)
    output = (preact * sigm).astype(jnp.bfloat16)
    grad_pre = (cotangent.astype(jnp.float32) * sigm * (1.0 + preact * (1.0 - sigm))).astype(
        jnp.bfloat16
    )
    part_self = jnp.einsum("nf,nh->fh", features, grad_pre, preferred_element_type=jnp.float32)
    part_neigh = jnp.einsum("nf,nh->fh", agg, grad_pre, preferred_element_type=jnp.float32)
    grad_own = jnp.einsum("nh,fh->nf", grad_pre, w_self, preferred_element_type=jnp.float32)
    grad_agg = jnp.einsum("nh,fh->nf", grad_pre, w_neigh, preferred_element_type=jnp.float32)
    grad_agg = (grad_agg / degree.reshape(-1)[:, None]).astype(jnp.bfloat16)
    picked = grad_agg.reshape(block_count, tile_size, width)[tile_tgt]
    backward = jnp.einsum("tif,tij->tfj", picked, tile_vals, preferred_element_type=jnp.float32)
    grad_source = jnp.einsum("st,tfj->sfj", to_source, backward, precision=lax.Precision.HIGHEST)
    remote = grad_source[block_count:].transpose(0, 2, 1).reshape(-1, width).astype(jnp.bfloat16)
    if table_bytes <= PLACE_LIMIT:
        returned = swap(remote, place, keep)
    else:
        remote = remote.reshape(n_dom + n_grp, bnd, width)
        ret_dom, ret_grp = exchange(remote[:n_dom], remote[n_dom:])
        returned = jnp.concatenate([ret_dom.reshape(-1, width), ret_grp.reshape(-1, width)])
    grad_self, grad_neigh = weight_sum(part_self, part_neigh)
    grad_total = grad_own + grad_source[:block_count].transpose(0, 2, 1).reshape(node_count, width)
    grad_total = grad_total + lax.dot_general(
        pick, returned, (((0,), (0,)), ((), ())), preferred_element_type=jnp.float32
    )
    return (output, grad_total.astype(jnp.bfloat16), grad_self, grad_neigh)


def solution(mesh):
    return jax.shard_map(
        per_device,
        mesh=mesh,
        in_specs=(
            P(("dom", "grp"), None),
            P(("dom", "grp"), None, None),
            P(("dom", "grp"), None, None),
            P(("dom", "grp"), None, None),
            P(("dom", "grp")),
            P(("dom", "grp")),
            P(("dom", "grp")),
            P(),
            P(),
            P(("dom", "grp"), None),
        ),
        out_specs=(P(("dom", "grp"), None), P(("dom", "grp"), None), P(), P()),
        check_vma=False,
    )
```

```python
import jax
import jax.numpy as jnp
from jax import lax
from jax.sharding import PartitionSpec as P


def weight_sum(part_self, part_neigh, stacked=None):
    axes = ("dom", "grp")
    peers = lax.psum(1, axes)
    rows = part_self.shape[0]
    if stacked is None:
        stacked = jnp.concatenate([part_self, part_neigh], axis=0)
    if stacked.shape[0] % (8 * peers) == 0:
        chunks = stacked.reshape(peers, -1, stacked.shape[1])
        mine = jnp.sum(lax.all_to_all(chunks, axes, 0, 0, tiled=True), axis=0, keepdims=True)
        total = lax.all_to_all(jnp.broadcast_to(mine, chunks.shape), axes, 0, 0, tiled=True)
        total = total.reshape(stacked.shape)
        return total[:rows], total[rows:]
    flat = stacked.reshape(-1)
    pad = (-flat.shape[0]) % peers
    chunks = jnp.pad(flat, (0, pad)).reshape(peers, -1)
    mine = jnp.sum(lax.all_to_all(chunks, axes, 0, 0, tiled=True), axis=0, keepdims=True)
    spread = jnp.broadcast_to(mine, chunks.shape)
    total = lax.all_to_all(spread, axes, 0, 0, tiled=True).reshape(-1)
    total = total[: flat.shape[0]].reshape(stacked.shape)
    return total[:rows], total[rows:]


def exchange(dom_part, grp_part):
    axes = ("dom", "grp")
    n_dom, n_grp = dom_part.shape[0], grp_part.shape[0]
    a = lax.axis_index("dom")
    b = lax.axis_index("grp")
    cell = dom_part.shape[1:]
    buf = jnp.zeros((n_dom, n_grp) + cell, dom_part.dtype)
    buf = lax.dynamic_update_slice_in_dim(buf, dom_part[:, None], b, axis=1)
    buf = lax.dynamic_update_slice_in_dim(buf, grp_part[None], a, axis=0)
    got = lax.all_to_all(buf.reshape((n_dom * n_grp,) + cell), axes, 0, 0, tiled=True)
    got = got.reshape((n_dom, n_grp) + cell)
    from_dom = lax.dynamic_index_in_dim(got, b, axis=1, keepdims=False)
    own_dom = lax.dynamic_index_in_dim(dom_part, a, axis=0, keepdims=True)
    from_dom = lax.dynamic_update_slice_in_dim(from_dom, own_dom, a, axis=0)
    from_grp = lax.dynamic_index_in_dim(got, a, axis=0, keepdims=False)
    return from_dom, from_grp


def one_hot_rows(index, count):
    hot = index[..., None] == jnp.arange(count, dtype=jnp.int32)
    return hot.astype(jnp.bfloat16).reshape(-1, count)


PLACE_LIMIT = 4 << 20


def placement(n_dom, n_grp, bnd):
    a = lax.axis_index("dom")
    b = lax.axis_index("grp")
    blk = jnp.arange(n_dom + n_grp, dtype=jnp.int32)
    cell = jnp.where(blk < n_dom, blk * n_grp + b, a * n_grp + (blk - n_dom))
    local = blk == a
    cell = jnp.where(local, -1, cell)
    col = cell[:, None] * bnd + jnp.arange(bnd, dtype=jnp.int32)[None, :]
    place = one_hot_rows(col, n_dom * n_grp * bnd)
    keep = jnp.broadcast_to(local[:, None], (n_dom + n_grp, bnd)).reshape(-1, 1)
    return place, keep


def swap(table, place, keep):
    peers = lax.psum(1, ("dom", "grp"))
    buf = lax.dot_general(place, table, (((0,), (0,)), ((), ())), preferred_element_type=jnp.float32)
    buf = buf.astype(table.dtype).reshape(peers, -1, table.shape[1])
    got = lax.all_to_all(buf, ("dom", "grp"), 0, 0, tiled=True).reshape(-1, table.shape[1])
    back = jnp.dot(place, got, preferred_element_type=jnp.float32).astype(table.dtype)
    return jnp.where(keep, table, back)


def per_device(
    features,
    send_dom,
    send_grp,
    tile_vals,
    tile_tgt,
    tile_src,
    tile_count,
    w_self,
    w_neigh,
    cotangent,
):
    tile_size = tile_vals.shape[1]
    width = features.shape[1]
    node_count = features.shape[0]
    block_count = node_count // tile_size
    dom_index = send_dom[0]
    grp_index = send_grp[0]
    n_dom, bnd = dom_index.shape
    n_grp = grp_index.shape[0]
    pick = one_hot_rows(jnp.concatenate([dom_index, grp_index], axis=0), node_count)
    sent = jnp.dot(pick, features, preferred_element_type=jnp.float32).astype(jnp.bfloat16)
    table_bytes = n_dom * n_grp * bnd * (n_dom + n_grp) * bnd * 2
    if table_bytes <= PLACE_LIMIT:
        place, keep = placement(n_dom, n_grp, bnd)
        got = swap(sent, place, keep)
        recv_dom, recv_grp = got[: n_dom * bnd], got[n_dom * bnd :]
    else:
        sent = sent.reshape(n_dom + n_grp, bnd, width)
        recv_dom, recv_grp = exchange(sent[:n_dom], sent[n_dom:])
    source = jnp.concatenate(
        [features, recv_dom.reshape(-1, width), recv_grp.reshape(-1, width)], axis=0
    )
    source = source.reshape(-1, tile_size, width)
    source_count = source.shape[0]
    slot_count = tile_vals.shape[0]
    usable = jnp.arange(slot_count, dtype=jnp.int32) < tile_count[0]
    to_target = (
        (tile_tgt[None, :] == jnp.arange(block_count, dtype=jnp.int32)[:, None]) & usable[None, :]
    ).astype(jnp.float32)
    to_source = (
        (tile_src[None, :] == jnp.arange(source_count, dtype=jnp.int32)[:, None]) & usable[None, :]
    ).astype(jnp.float32)
    products = jnp.einsum(
        "tjf,tij->tfi", source[tile_src], tile_vals, preferred_element_type=jnp.float32
    )
    summed = jnp.einsum("bt,tfi->bif", to_target, products, precision=lax.Precision.HIGHEST)
    unit_column = jnp.ones((tile_size,), jnp.bfloat16)
    row_sums = jnp.einsum("tij,j->ti", tile_vals, unit_column, preferred_element_type=jnp.float32)
    degree = jnp.dot(to_target, row_sums, precision=lax.Precision.HIGHEST)
    agg = (summed / degree[:, :, None]).reshape(node_count, width).astype(jnp.bfloat16)
    preact = jnp.dot(features, w_self, preferred_element_type=jnp.float32) + jnp.dot(
        agg, w_neigh, preferred_element_type=jnp.float32
    )
    sigm = jax.nn.sigmoid(preact)
    output = (preact * sigm).astype(jnp.bfloat16)
    grad_pre = (cotangent.astype(jnp.float32) * sigm * (1.0 + preact * (1.0 - sigm))).astype(
        jnp.bfloat16
    )
    part_self = jnp.einsum("nf,nh->fh", features, grad_pre, preferred_element_type=jnp.float32)
    part_neigh = jnp.einsum("nf,nh->fh", agg, grad_pre, preferred_element_type=jnp.float32)
    both = jnp.einsum(
        "nh,fh->nf", grad_pre, jnp.concatenate([w_self, w_neigh], axis=0),
        preferred_element_type=jnp.float32,
    )
    grad_own, grad_agg = both[:, :width], both[:, width:]
    grad_agg = (grad_agg / degree.reshape(-1)[:, None]).astype(jnp.bfloat16)
    picked = grad_agg.reshape(block_count, tile_size, width)[tile_tgt]
    backward = jnp.einsum("tif,tij->tfj", picked, tile_vals, preferred_element_type=jnp.float32)
    grad_source = jnp.einsum("st,tfj->sfj", to_source, backward, precision=lax.Precision.HIGHEST)
    remote = grad_source[block_count:].transpose(0, 2, 1).reshape(-1, width).astype(jnp.bfloat16)
    if table_bytes <= PLACE_LIMIT:
        returned = swap(remote, place, keep)
    else:
        remote = remote.reshape(n_dom + n_grp, bnd, width)
        ret_dom, ret_grp = exchange(remote[:n_dom], remote[n_dom:])
        returned = jnp.concatenate([ret_dom.reshape(-1, width), ret_grp.reshape(-1, width)])
    grad_self, grad_neigh = weight_sum(part_self, part_neigh)
    grad_total = grad_own + grad_source[:block_count].transpose(0, 2, 1).reshape(node_count, width)
    grad_total = grad_total + lax.dot_general(
        pick, returned, (((0,), (0,)), ((), ())), preferred_element_type=jnp.float32
    )
    return (output, grad_total.astype(jnp.bfloat16), grad_self, grad_neigh)


def solution(mesh):
    return jax.shard_map(
        per_device,
        mesh=mesh,
        in_specs=(
            P(("dom", "grp"), None),
            P(("dom", "grp"), None, None),
            P(("dom", "grp"), None, None),
            P(("dom", "grp"), None, None),
            P(("dom", "grp")),
            P(("dom", "grp")),
            P(("dom", "grp")),
            P(),
            P(),
            P(("dom", "grp"), None),
        ),
        out_specs=(P(("dom", "grp"), None), P(("dom", "grp"), None), P(), P()),
        check_vma=False,
    )
```
